32 devices in a mesh: seq: 8 (over z, y), head: 4 (over x, core).
Axes of the slice: x: 2, y: 2, z: 4, core: 2. Of those that a mesh axis runs over, the one named last changes fastest.
Arguments:
- queries: bfloat16 [8, 32, 128, 128], P(None, None, 'head'), may hold values from -6 to 6
- cache_keys: bfloat16 [8, 16384, 8, 128], P(None, 'seq', 'head'), may hold values from -6 to 6
- cache_values: bfloat16 [8, 16384, 8, 128], P(None, 'seq', 'head'), may hold values from -9 to 9
- lengths: int32 [8], replicated, may hold values from 4096 to 16384, as said below
- parents: int32 [8, 32], replicated, may hold values from 0 to 30, as said below
- draft_keys: bfloat16 [8, 32, 8, 128], P(None, 'seq', 'head'), may hold values from -14 to 14
- draft_values: bfloat16 [8, 32, 8, 128], P(None, 'seq', 'head'), may hold values from -9 to 9
- out_weight: bfloat16 [16384, 16384], P('head', 'seq'), may hold values from -0.0625 to 0.0625
Outputs:
- projected: bfloat16 [256, 16384], P(None, ('seq', 'head'))
The draws below stay inside these ranges and needn't reach their ends.
Inputs may be any that keep to these rules, and one draw needn't show every extreme that they name: parents[r, 0] = 0 (the root) and 0 <= parents[r, i] < i for every other token. `lengths`: some request fills its whole cache.
All inputs are finite; a program needn't handle non-finite values.
Results may differ from the reference program's by a relative error of at most 0.007.
Values may be sent and summed in bfloat16 or wider, within the bound.
No kernel may reach another device: no remote copies, remote signals or barrier semaphores. Data moves between devices by JAX's collectives and lax.ppermute only.
A program may use at most 192 MiB of HBM per device.

```python
import jax
import jax.numpy as jnp
from jax import lax

D = 16384
QH = 128
KVH = 8
DH = 128
REQS = 8
CACHE_DEV = 2048
CTX = 16384
TREE = 32


def draw_queries(key, part):
    base = jax.random.normal(jax.random.fold_in(key, 1), (REQS, TREE, QH, DH), dtype=jnp.float32)
    base = jnp.clip(base, -6.0, 6.0)
    return base.astype(jnp.bfloat16)


def draw_cache_keys(key, part):
    base = jax.random.normal(jax.random.fold_in(key, 3), (REQS, CTX, KVH, DH), dtype=jnp.float32)
    base = jnp.clip(base, -6.0, 6.0)
    return base.astype(jnp.bfloat16)


def draw_cache_values(key, part):
    offset = jax.random.normal(jax.random.fold_in(key, 5), (REQS, CTX // CACHE_DEV, KVH, DH), dtype=jnp.float32) * 1.5
    offset = jnp.repeat(offset, CACHE_DEV, axis=1)
    noise = jax.random.normal(jax.random.fold_in(key, 6), (REQS, CTX, KVH, DH), dtype=jnp.float32)
    values = noise + offset
    return jnp.clip(values, -9.0, 9.0).astype(jnp.bfloat16)


def draw_lengths(key, part):
    filled = jax.random.randint(jax.random.fold_in(key, 11), (REQS,), CTX // 4, CTX + 1, dtype=jnp.int32)
    pick = jax.random.randint(jax.random.fold_in(key, 12), (), 0, REQS, dtype=jnp.int32)
    return jnp.where(jnp.arange(REQS, dtype=jnp.int32) == pick, CTX, filled).astype(jnp.int32)


def draw_parents(key, part):
    tokens = jnp.arange(TREE, dtype=jnp.int32)
    back = jax.random.randint(jax.random.fold_in(key, 13), (REQS, TREE), 0, 3, dtype=jnp.int32)
    linked = jnp.maximum(tokens[None, :] - 1 - back, 0)
    return jnp.where(tokens[None, :] == 0, 0, linked).astype(jnp.int32)


def spiked(array, stream_key, source, target, blocks, factor):
    def block_of(dim):
        return (jnp.arange(array.shape[dim]) // (array.shape[dim] // blocks)).reshape((-1,) + (1,) * (array.ndim - 1 - dim))

    one_side = jax.random.permutation(stream_key, blocks)[block_of(target)]
    second = (block_of(target) + blocks // 2) % blocks
    return jnp.where((block_of(source) == one_side) | (block_of(source) == second), factor * array, array)


def levels(key, dims, cuts, least, largest):
    loudness, own = 1.0, jax.random.fold_in(key, 6)
    for axis_at, blocks in cuts:
        steps = jnp.exp(jax.random.uniform(jax.random.fold_in(own, axis_at), (blocks,), jnp.float32, least / len(cuts), largest / len(cuts)))
        loudness = loudness * jnp.repeat(steps, dims[axis_at] // blocks).reshape([-1 if axis == axis_at else 1 for axis in range(len(dims))])
    return loudness


def gaussian(rng, dims, spread, limit, cuts=(), held_as=jnp.bfloat16):
    drawn = spread * jax.random.normal(rng, dims, jnp.float32)
    if cuts:
        drawn = drawn * levels(rng, dims, cuts, -0.22, 0.18)
    return jnp.clip(drawn, -limit, limit).astype(held_as)


def bell_draw_with(rng, extent, deviation, bound, split, heavy, kind=jnp.bfloat16):
    result = deviation * jax.random.normal(rng, extent, jnp.float32)
    if split:
        result = result * levels(rng, extent, split, -0.22, 0.18)
    return jnp.clip(spiked(result, jax.random.fold_in(rng, 3), *heavy), -bound, bound).astype(kind)


def setup_inputs(seed: int = 0) -> dict:
    keys = jax.random.split(jax.random.key(seed), 9)
    queries = draw_queries(jax.random.fold_in(keys[8], 71), 0)
    cache_keys = draw_cache_keys(jax.random.fold_in(keys[8], 71), 0)
    cache_values = draw_cache_values(jax.random.fold_in(keys[8], 71), 0)
    lengths = draw_lengths(jax.random.fold_in(keys[8], 71), 0)
    parents = draw_parents(jax.random.fold_in(keys[8], 71), 0)
    draft_keys = gaussian(keys[5], (REQS, TREE, KVH, DH), 3.5, 14.0, ((1, 8), (2, 4)))
    draft_values = gaussian(keys[6], (REQS, TREE, KVH, DH), 1.5, 9.0, ((1, 8), (2, 4)))
    out_weight = bell_draw_with(keys[7], (QH * DH, D), (QH * DH) ** -0.5, 0.0625, ((0, 4), (1, 8)), (0, 1, 8, 2.0))
    return {"queries": queries, "cache_keys": cache_keys, "cache_values": cache_values, "lengths": lengths, "parents": parents, "draft_keys": draft_keys, "draft_values": draft_values, "out_weight": out_weight}


NEG_BIG = -1e30


def ancestry(parents):
    tree_len = parents.shape[1]
    columns = jnp.arange(tree_len, dtype=jnp.int32)
    linked = (parents[:, :, None] == columns[None, None, :]) | (columns[:, None] == columns[None, :])[None, :, :]
    reach = linked.astype(jnp.float32)
    for step in range(tree_len.bit_length()):
        reach = jnp.minimum(jnp.einsum("rij,rjk->rik", reach, reach, precision=lax.Precision.HIGHEST), 1.0)
    return reach > 0.5


def head_attend(inputs):
    query_rows, key_rows, value_rows, draft_key, draft_value, valid_keys, tree_mask = inputs
    scale_factor = DH ** -0.5
    all_keys = jnp.concatenate([key_rows, draft_key], axis=0).astype(jnp.float32)
    all_values = jnp.concatenate([value_rows, draft_value], axis=0).astype(jnp.float32)
    keep = jnp.concatenate([jnp.broadcast_to(valid_keys[None, :], (TREE, CTX)), tree_mask], axis=1)
    scores = jnp.einsum("tgd,sd->tgs", query_rows.astype(jnp.float32), all_keys) * scale_factor
    scores = jnp.where(keep[:, None, :], scores, NEG_BIG)
    row_top = jnp.max(scores, axis=-1, keepdims=True)
    weights = jnp.where(keep[:, None, :], jnp.exp(scores - row_top), 0.0)
    total = jnp.sum(weights, axis=-1)
    rounded = lax.optimization_barrier(weights.astype(jnp.bfloat16)).astype(jnp.float32)
    numerator = jnp.einsum("tgs,sd->tgd", rounded, all_values)
    return (numerator / total[:, :, None]).astype(jnp.bfloat16)


def request_attend(inputs):
    query_req, key_req, value_req, draft_key, draft_value, length_req, tree_mask = inputs
    group = QH // KVH
    query_heads = jnp.transpose(query_req.reshape(TREE, KVH, group, DH), (1, 0, 2, 3))
    valid_keys = jnp.arange(CTX, dtype=jnp.int32) < length_req
    per_head = lax.map(
        lambda pieces: head_attend((pieces[0], pieces[1], pieces[2], pieces[3], pieces[4], valid_keys, tree_mask)),
        (query_heads, jnp.transpose(key_req, (1, 0, 2)), jnp.transpose(value_req, (1, 0, 2)),
         jnp.transpose(draft_key, (1, 0, 2)), jnp.transpose(draft_value, (1, 0, 2))))
    return jnp.transpose(per_head, (1, 0, 2, 3)).reshape(TREE, QH * DH)


def reference(queries, cache_keys, cache_values, lengths, parents, draft_keys, draft_values, out_weight):
    tree_mask = ancestry(parents)
    attended = lax.map(request_attend, (queries, cache_keys, cache_values, draft_keys, draft_values, lengths, tree_mask))
    attended = attended.reshape(REQS * TREE, QH * DH)
    return jnp.dot(attended, out_weight, preferred_element_type=jnp.float32).astype(jnp.bfloat16)
```

```python
import functools

import jax
import jax.numpy as jnp
from jax import lax
from jax.experimental import pallas as pl
from jax.experimental.pallas import tpu as pltpu
from jax.sharding import PartitionSpec as P

NEG_BIG = -1e30
DRAFT_PAD = 128
ROW_TOKENS = 8


def ancestry(parents):
    tree_len = parents.shape[1]
    columns = jnp.arange(tree_len, dtype=jnp.int32)
    linked = (parents[:, :, None] == columns[None, None, :]) | (
        columns[:, None] == columns[None, :]
    )[None, :, :]
    reach = linked.astype(jnp.float32)
    for step in range(tree_len.bit_length()):
        reach = jnp.minimum(
            jnp.einsum("rij,rjk->rik", reach, reach, precision=lax.Precision.HIGHEST), 1.0
        )
    return reach > 0.5


def attend_kernel(lens_ref, q_ref, k_ref, v_ref, dk_ref, dv_ref, dmask_ref,
                  num_ref, top_ref, tot_ref, *, group, local_kv):
    r = pl.program_id(0)
    length = lens_ref[r]
    head_size = q_ref.shape[-1]
    scale_factor = head_size ** (-0.5)
    rows = ROW_TOKENS * group
    dims = (((1,), (1,)), ((), ()))

    for kv in range(local_kv):
        keys = k_ref[:, kv, :]
        values = v_ref[:, kv, :]
        draft_key = dk_ref[kv]
        draft_value = dv_ref[kv]
        heads = pl.ds(kv * group, group)

        def chunk(i, carry, keys=keys, values=values, draft_key=draft_key,
                  draft_value=draft_value, heads=heads, kv=kv):
            t0 = pl.multiple_of(i * ROW_TOKENS, ROW_TOKENS)
            q = q_ref[pl.ds(t0, ROW_TOKENS), heads, :].reshape(rows, head_size)
            scores = (
                lax.dot_general(q, keys, dims, preferred_element_type=jnp.float32) * scale_factor
            )
            column = lax.broadcasted_iota(jnp.int32, scores.shape, 1)
            scores = jnp.where(column < length, scores, NEG_BIG)
            draft_scores = (
                lax.dot_general(q, draft_key, dims, preferred_element_type=jnp.float32)
                * scale_factor
            )
            draft_keep = dmask_ref[pl.ds(t0, ROW_TOKENS)]
            draft_keep = jnp.broadcast_to(
                draft_keep[:, None, :], (ROW_TOKENS, group, DRAFT_PAD)
            ).reshape(rows, DRAFT_PAD)
            draft_scores = jnp.where(draft_keep > 0.5, draft_scores, NEG_BIG)
            top = jnp.maximum(
                jnp.max(scores, axis=-1, keepdims=True),
                jnp.max(draft_scores, axis=-1, keepdims=True),
            )
            safe_top = jnp.maximum(top, NEG_BIG * 0.1)
            weight = jnp.exp(scores - safe_top)
            draft_weight = jnp.exp(draft_scores - safe_top)
            total = jnp.sum(weight, axis=-1, keepdims=True) + jnp.sum(
                draft_weight, axis=-1, keepdims=True
            )
            numerator = jnp.dot(
                weight.astype(jnp.bfloat16), values, preferred_element_type=jnp.float32
            ) + jnp.dot(
                draft_weight.astype(jnp.bfloat16), draft_value,
                preferred_element_type=jnp.float32,
            )
            num_ref[pl.ds(t0, ROW_TOKENS), heads, :] = numerator.reshape(
                ROW_TOKENS, group, head_size
            )
            r0 = pl.multiple_of(i * rows, rows)
            top_ref[kv, pl.ds(r0, rows), :] = jnp.broadcast_to(safe_top, (rows, 128))
            tot_ref[kv, pl.ds(r0, rows), :] = jnp.broadcast_to(total, (rows, 128))
            return carry

        lax.fori_loop(0, q_ref.shape[0] // ROW_TOKENS, chunk, 0)


def attend(local_len, queries, cache_keys, cache_values, draft_k, draft_v, draft_mask):
    requests, tree_len, local_heads, head_size = queries.shape
    shard_len = cache_keys.shape[1]
    local_kv = cache_keys.shape[2]
    group = local_heads // local_kv
    kernel = functools.partial(attend_kernel, group=group, local_kv=local_kv)
    stats = jax.ShapeDtypeStruct((requests, local_kv, tree_len * group, 128), jnp.float32)
    grid_spec = pltpu.PrefetchScalarGridSpec(
        num_scalar_prefetch=1,
        grid=(requests,),
        in_specs=[
            pl.BlockSpec((None, tree_len, local_heads, head_size), lambda r, lens: (r, 0, 0, 0)),
            pl.BlockSpec((None, shard_len, local_kv, head_size), lambda r, lens: (r, 0, 0, 0)),
            pl.BlockSpec((None, shard_len, local_kv, head_size), lambda r, lens: (r, 0, 0, 0)),
            pl.BlockSpec((None, local_kv, DRAFT_PAD, head_size), lambda r, lens: (r, 0, 0, 0)),
            pl.BlockSpec((None, local_kv, DRAFT_PAD, head_size), lambda r, lens: (r, 0, 0, 0)),
            pl.BlockSpec((None, tree_len, DRAFT_PAD), lambda r, lens: (r, 0, 0)),
        ],
        out_specs=[
            pl.BlockSpec((None, tree_len, local_heads, head_size), lambda r, lens: (r, 0, 0, 0)),
            pl.BlockSpec((None, local_kv, tree_len * group, 128), lambda r, lens: (r, 0, 0, 0)),
            pl.BlockSpec((None, local_kv, tree_len * group, 128), lambda r, lens: (r, 0, 0, 0)),
        ],
    )
    flops = 4 * requests * tree_len * local_heads * (shard_len + DRAFT_PAD) * head_size
    return pl.pallas_call(
        kernel,
        grid_spec=grid_spec,
        out_shape=[
            jax.ShapeDtypeStruct(queries.shape, jnp.float32),
            stats,
            stats,
        ],
        compiler_params=pltpu.CompilerParams(
            dimension_semantics=("arbitrary",),
            vmem_limit_bytes=48 * 1024 * 1024,
        ),
        cost_estimate=pl.CostEstimate(
            flops=flops,
            transcendentals=requests * tree_len * local_heads * (shard_len + DRAFT_PAD),
            bytes_accessed=2 * cache_keys.size * 2 + queries.size * 2 + queries.size * 4,
        ),
    )(local_len, queries, cache_keys, cache_values, draft_k, draft_v, draft_mask)


def local(
    queries, cache_keys, cache_values, lengths, parents, draft_keys, draft_values, out_weight
):
    requests, tree_len, local_heads, head_size = queries.shape
    shard_len = cache_keys.shape[1]
    local_kv = cache_keys.shape[2]
    group = local_heads // local_kv
    draft_len = draft_keys.shape[1]
    seq_size = lax.axis_size("seq")
    seq_index = lax.axis_index("seq")
    tree_mask = ancestry(parents)
    local_len = jnp.clip(lengths - seq_index * shard_len, 0, shard_len).astype(jnp.int32)
    draft_mask = lax.dynamic_slice_in_dim(tree_mask, seq_index * draft_len, draft_len, 2)
    draft_mask = jnp.pad(
        draft_mask.astype(jnp.float32), ((0, 0), (0, 0), (0, DRAFT_PAD - draft_len))
    )
    pad = ((0, 0), (0, 0), (0, DRAFT_PAD - draft_len), (0, 0))
    draft_k = jnp.pad(jnp.transpose(draft_keys, (0, 2, 1, 3)), pad)
    draft_v = jnp.pad(jnp.transpose(draft_values, (0, 2, 1, 3)), pad)
    numerator, top, total = attend(
        local_len, queries, cache_keys, cache_values, draft_k, draft_v, draft_mask
    )

    def per_head(stat):
        stat = stat[..., 0].reshape(requests, local_kv, tree_len, group)
        return jnp.transpose(stat, (0, 2, 1, 3)).reshape(requests, tree_len, local_heads)

    top = per_head(top)
    total = per_head(total)
    all_top = lax.all_gather(top, "seq")
    common_top = jnp.max(all_top, axis=0)
    scaling = jnp.exp(top - common_top)
    scaled_total = jnp.pad(
        (total * scaling)[:, :, None, :], ((0, 0), (0, 0), (0, 0), (0, head_size - local_heads))
    )
    packed = jnp.concatenate([numerator * scaling[..., None], scaled_total], axis=2)
    packed = packed.reshape(requests * tree_len, local_heads + 1, head_size)
    mine = lax.psum_scatter(packed, "seq", scatter_dimension=0, tiled=True)
    mine_total = mine[:, local_heads, :local_heads]
    mine_attended = (mine[:, :local_heads, :] / mine_total[..., None]).astype(jnp.bfloat16)
    attended = lax.all_gather(mine_attended, "seq", axis=0, tiled=True)
    attended = attended.reshape(requests * tree_len, local_heads * head_size)
    terms = jnp.dot(attended, out_weight, preferred_element_type=jnp.float32)
    return lax.psum_scatter(terms, "head", scatter_dimension=1, tiled=True).astype(jnp.bfloat16)


def solution(mesh):
    return jax.shard_map(
        local,
        mesh=mesh,
        in_specs=(
            P(None, None, "head", None),
            P(None, "seq", "head", None),
            P(None, "seq", "head", None),
            P(),
            P(),
            P(None, "seq", "head", None),
            P(None, "seq", "head", None),
            P("head", "seq"),
        ),
        out_specs=P(None, ("seq", "head")),
        check_vma=False,
    )
```

```python
import functools

import jax
import jax.numpy as jnp
from jax import lax
from jax.experimental import pallas as pl
from jax.experimental.pallas import tpu as pltpu
from jax.sharding import PartitionSpec as P

NEG_BIG = -1e30
DRAFT_PAD = 128
ROW_TOKENS = 8


def ancestry(parents):
    tree_len = parents.shape[1]
    columns = jnp.arange(tree_len, dtype=jnp.int32)
    linked = (parents[:, :, None] == columns[None, None, :]) | (
        columns[:, None] == columns[None, :]
    )[None, :, :]
    reach = linked.astype(jnp.float32)
    for step in range(tree_len.bit_length()):
        reach = jnp.minimum(
            jnp.einsum("rij,rjk->rik", reach, reach, precision=lax.Precision.HIGHEST), 1.0
        )
    return reach > 0.5


def attend_kernel(lens_ref, q_ref, k_ref, v_ref, dk_ref, dv_ref, dmask_ref,
                  num_ref, top_ref, tot_ref, *, group, local_kv):
    r = pl.program_id(0)
    length = lens_ref[r]
    head_size = q_ref.shape[-1]
    scale_factor = head_size ** (-0.5)
    rows = ROW_TOKENS * group
    dims = (((1,), (1,)), ((), ()))

    for kv in range(local_kv):
        keys = k_ref[kv]
        values = v_ref[kv]
        draft_key = dk_ref[kv]
        draft_value = dv_ref[kv]
        heads = pl.ds(kv * group, group)

        def chunk(i, carry, keys=keys, values=values, draft_key=draft_key,
                  draft_value=draft_value, heads=heads, kv=kv):
            t0 = pl.multiple_of(i * ROW_TOKENS, ROW_TOKENS)
            q = q_ref[pl.ds(t0, ROW_TOKENS), heads, :].reshape(rows, head_size)
            scores = (
                lax.dot_general(q, keys, dims, preferred_element_type=jnp.float32) * scale_factor
            )
            column = lax.broadcasted_iota(jnp.int32, scores.shape, 1)
            scores = jnp.where(column < length, scores, NEG_BIG)
            draft_scores = (
                lax.dot_general(q, draft_key, dims, preferred_element_type=jnp.float32)
                * scale_factor
            )
            draft_keep = dmask_ref[pl.ds(t0, ROW_TOKENS)]
            draft_keep = jnp.broadcast_to(
                draft_keep[:, None, :], (ROW_TOKENS, group, DRAFT_PAD)
            ).reshape(rows, DRAFT_PAD)
            draft_scores = jnp.where(draft_keep > 0.5, draft_scores, NEG_BIG)
            top = jnp.maximum(
                jnp.max(scores, axis=-1, keepdims=True),
                jnp.max(draft_scores, axis=-1, keepdims=True),
            )
            safe_top = jnp.maximum(top, NEG_BIG * 0.1)
            weight = jnp.exp(scores - safe_top)
            draft_weight = jnp.exp(draft_scores - safe_top)
            total = jnp.sum(weight, axis=-1, keepdims=True) + jnp.sum(
                draft_weight, axis=-1, keepdims=True
            )
            numerator = jnp.dot(
                weight.astype(jnp.bfloat16), values, preferred_element_type=jnp.float32
            ) + jnp.dot(
                draft_weight.astype(jnp.bfloat16), draft_value,
                preferred_element_type=jnp.float32,
            )
            num_ref[pl.ds(t0, ROW_TOKENS), heads, :] = numerator.reshape(
                ROW_TOKENS, group, head_size
            )
            r0 = pl.multiple_of(i * rows, rows)
            top_ref[kv, pl.ds(r0, rows), :] = jnp.broadcast_to(safe_top, (rows, 128))
            tot_ref[kv, pl.ds(r0, rows), :] = jnp.broadcast_to(total, (rows, 128))
            return carry

        lax.fori_loop(0, q_ref.shape[0] // ROW_TOKENS, chunk, 0)


def attend(local_len, queries, cache_keys, cache_values, draft_k, draft_v, draft_mask):
    requests, tree_len, local_heads, head_size = queries.shape
    local_kv = cache_keys.shape[1]
    shard_len = cache_keys.shape[2]
    group = local_heads // local_kv
    kernel = functools.partial(attend_kernel, group=group, local_kv=local_kv)
    stats = jax.ShapeDtypeStruct((requests, local_kv, tree_len * group, 128), jnp.float32)
    grid_spec = pltpu.PrefetchScalarGridSpec(
        num_scalar_prefetch=1,
        grid=(requests,),
        in_specs=[
            pl.BlockSpec((None, tree_len, local_heads, head_size), lambda r, lens: (r, 0, 0, 0)),
            pl.BlockSpec((None, local_kv, shard_len, head_size), lambda r, lens: (r, 0, 0, 0)),
            pl.BlockSpec((None, local_kv, shard_len, head_size), lambda r, lens: (r, 0, 0, 0)),
            pl.BlockSpec((None, local_kv, DRAFT_PAD, head_size), lambda r, lens: (r, 0, 0, 0)),
            pl.BlockSpec((None, local_kv, DRAFT_PAD, head_size), lambda r, lens: (r, 0, 0, 0)),
            pl.BlockSpec((None, tree_len, DRAFT_PAD), lambda r, lens: (r, 0, 0)),
        ],
        out_specs=[
            pl.BlockSpec((None, tree_len, local_heads, head_size), lambda r, lens: (r, 0, 0, 0)),
            pl.BlockSpec((None, local_kv, tree_len * group, 128), lambda r, lens: (r, 0, 0, 0)),
            pl.BlockSpec((None, local_kv, tree_len * group, 128), lambda r, lens: (r, 0, 0, 0)),
        ],
    )
    flops = 4 * requests * tree_len * local_heads * (shard_len + DRAFT_PAD) * head_size
    return pl.pallas_call(
        kernel,
        grid_spec=grid_spec,
        out_shape=[
            jax.ShapeDtypeStruct(queries.shape, jnp.float32),
            stats,
            stats,
        ],
        compiler_params=pltpu.CompilerParams(
            dimension_semantics=("arbitrary",),
            vmem_limit_bytes=48 * 1024 * 1024,
        ),
        cost_estimate=pl.CostEstimate(
            flops=flops,
            transcendentals=requests * tree_len * local_heads * (shard_len + DRAFT_PAD),
            bytes_accessed=2 * cache_keys.size * 2 + queries.size * 2 + queries.size * 4,
        ),
    )(local_len, queries, cache_keys, cache_values, draft_k, draft_v, draft_mask)


def local(
    queries, cache_keys, cache_values, lengths, parents, draft_keys, draft_values, out_weight
):
    requests, tree_len, local_heads, head_size = queries.shape
    shard_len = cache_keys.shape[1]
    local_kv = cache_keys.shape[2]
    group = local_heads // local_kv
    draft_len = draft_keys.shape[1]
    seq_size = lax.axis_size("seq")
    seq_index = lax.axis_index("seq")
    tree_mask = ancestry(parents)
    local_len = jnp.clip(lengths - seq_index * shard_len, 0, shard_len).astype(jnp.int32)
    draft_mask = lax.dynamic_slice_in_dim(tree_mask, seq_index * draft_len, draft_len, 2)
    draft_mask = jnp.pad(
        draft_mask.astype(jnp.float32), ((0, 0), (0, 0), (0, DRAFT_PAD - draft_len))
    )
    pad = ((0, 0), (0, 0), (0, DRAFT_PAD - draft_len), (0, 0))
    draft_k = jnp.pad(jnp.transpose(draft_keys, (0, 2, 1, 3)), pad)
    draft_v = jnp.pad(jnp.transpose(draft_values, (0, 2, 1, 3)), pad)
    numerator, top, total = attend(
        local_len, queries, jnp.transpose(cache_keys, (0, 2, 1, 3)),
        jnp.transpose(cache_values, (0, 2, 1, 3)), draft_k, draft_v, draft_mask
    )

    def per_head(stat):
        stat = stat[..., 0].reshape(requests, local_kv, tree_len, group)
        return jnp.transpose(stat, (0, 2, 1, 3)).reshape(requests, tree_len, local_heads)

    seq_size = lax.axis_size("seq")
    rows = requests * tree_len
    top = per_head(top)
    total = per_head(total)
    stats = jnp.concatenate(
        [top, total, jnp.zeros((requests, tree_len, head_size - 2 * local_heads), jnp.float32)],
        axis=-1,
    )
    packed = jnp.concatenate([numerator, stats[:, :, None, :]], axis=2)
    packed = packed.reshape(seq_size, rows // seq_size, local_heads + 1, head_size)
    got = lax.all_to_all(packed, "seq", 0, 0, tiled=True)
    got_stats = got[:, :, local_heads, :]
    got_common = got_stats[..., :local_heads]
    got_total = got_stats[..., local_heads:2 * local_heads]
    peak = jnp.max(got_common, axis=0)
    scaling = jnp.exp(got_common - peak)
    summed_total = jnp.sum(got_total * scaling, axis=0)
    summed = jnp.sum(got[:, :, :local_heads, :] * scaling[..., None], axis=0)
    mine_attended = (summed / summed_total[..., None]).astype(jnp.bfloat16)
    attended = lax.all_gather(mine_attended, "seq", axis=0, tiled=True)
    attended = attended.reshape(requests * tree_len, local_heads * head_size)
    terms = jnp.dot(attended, out_weight, preferred_element_type=jnp.float32)
    return lax.psum_scatter(terms, "head", scatter_dimension=1, tiled=True).astype(jnp.bfloat16)


def solution(mesh):
    return jax.shard_map(
        local,
        mesh=mesh,
        in_specs=(
            P(None, None, "head", None),
            P(None, "seq", "head", None),
            P(None, "seq", "head", None),
            P(),
            P(),
            P(None, "seq", "head", None),
            P(None, "seq", "head", None),
            P("head", "seq"),
        ),
        out_specs=P(None, ("seq", "head")),
        check_vma=False,
    )
```

```python
import functools

import jax
import jax.numpy as jnp
from jax import lax
from jax.experimental import pallas as pl
from jax.experimental.pallas import tpu as pltpu
from jax.sharding import PartitionSpec as P

NEG_BIG = -1e30
DRAFT_PAD = 128
ROW_TOKENS = 8
COLUMNS = 256


def ancestry(parents):
    tree_len = parents.shape[1]
    columns = jnp.arange(tree_len, dtype=jnp.int32)
    linked = (parents[:, :, None] == columns[None, None, :]) | (
        columns[:, None] == columns[None, :]
    )[None, :, :]
    reach = linked.astype(jnp.float32)
    for step in range(tree_len.bit_length()):
        reach = jnp.minimum(
            jnp.einsum("rij,rjk->rik", reach, reach, precision=lax.Precision.HIGHEST), 1.0
        )
    return reach > 0.5


def attend_kernel(lens_ref, q_ref, k_ref, v_ref, dk_ref, dv_ref, dmask_ref,
                  num_ref, top_ref, tot_ref, *, group, local_kv):
    r = pl.program_id(0)
    length = lens_ref[r]
    head_size = q_ref.shape[-1]
    shard_len = k_ref.shape[1]
    scale_factor = head_size ** (-0.5)
    rows = ROW_TOKENS * group
    dims = (((1,), (1,)), ((), ()))
    steps = shard_len // COLUMNS

    for kv in range(local_kv):
        heads = pl.ds(kv * group, group)

        def chunk(i, carry, kv=kv, heads=heads):
            t0 = pl.multiple_of(i * ROW_TOKENS, ROW_TOKENS)
            q = q_ref[pl.ds(t0, ROW_TOKENS), heads, :].reshape(rows, head_size)

            def scores_at(c):
                c0 = pl.multiple_of(c * COLUMNS, COLUMNS)
                keys = k_ref[kv, pl.ds(c0, COLUMNS), :]
                block = lax.dot_general(q, keys, dims, preferred_element_type=jnp.float32)

                def masked(block):
                    column = c0 + lax.broadcasted_iota(jnp.int32, block.shape, 1)
                    return jnp.where(column < length, block, NEG_BIG)

                return lax.cond(c0 + COLUMNS <= length, lambda b: b, masked, block), c0

            draft_scores = lax.dot_general(q, dk_ref[kv], dims, preferred_element_type=jnp.float32)
            draft_keep = dmask_ref[pl.ds(t0, ROW_TOKENS)]
            draft_keep = jnp.broadcast_to(
                draft_keep[:, None, :], (ROW_TOKENS, group, DRAFT_PAD)
            ).reshape(rows, DRAFT_PAD)
            draft_scores = jnp.where(draft_keep > 0.5, draft_scores, NEG_BIG)

            def find_top(c, top):
                block, _ = scores_at(c)
                return jnp.maximum(top, jnp.max(block, axis=-1, keepdims=True))

            top = lax.fori_loop(
                0, steps, find_top, jnp.max(draft_scores, axis=-1, keepdims=True), unroll=True
            )
            safe_top = jnp.maximum(top, NEG_BIG * 0.1)

            def accumulate(c, acc):
                total, numerator = acc
                block, c0 = scores_at(c)
                weight = jnp.exp((block - safe_top) * scale_factor)
                values = v_ref[kv, pl.ds(c0, COLUMNS), :]
                return (
                    total + jnp.sum(weight, axis=-1, keepdims=True),
                    numerator + jnp.dot(
                        weight.astype(jnp.bfloat16), values, preferred_element_type=jnp.float32
                    ),
                )

            draft_weight = jnp.exp((draft_scores - safe_top) * scale_factor)
            start = (
                jnp.sum(draft_weight, axis=-1, keepdims=True),
                jnp.dot(
                    draft_weight.astype(jnp.bfloat16), dv_ref[kv],
                    preferred_element_type=jnp.float32,
                ),
            )
            total, numerator = lax.fori_loop(0, steps, accumulate, start, unroll=True)
            num_ref[pl.ds(t0, ROW_TOKENS), heads, :] = numerator.reshape(
                ROW_TOKENS, group, head_size
            )
            r0 = pl.multiple_of(i * rows, rows)
            top_ref[kv, pl.ds(r0, rows), :] = jnp.broadcast_to(safe_top * scale_factor, (rows, 128))
            tot_ref[kv, pl.ds(r0, rows), :] = jnp.broadcast_to(total, (rows, 128))
            return carry

        lax.fori_loop(0, q_ref.shape[0] // ROW_TOKENS, chunk, 0)


def attend(local_len, queries, cache_keys, cache_values, draft_k, draft_v, draft_mask):
    requests, tree_len, local_heads, head_size = queries.shape
    local_kv = cache_keys.shape[1]
    shard_len = cache_keys.shape[2]
    group = local_heads // local_kv
    kernel = functools.partial(attend_kernel, group=group, local_kv=local_kv)
    stats = jax.ShapeDtypeStruct((requests, local_kv, tree_len * group, 128), jnp.float32)
    grid_spec = pltpu.PrefetchScalarGridSpec(
        num_scalar_prefetch=1,
        grid=(requests,),
        in_specs=[
            pl.BlockSpec((None, tree_len, local_heads, head_size), lambda r, lens: (r, 0, 0, 0)),
            pl.BlockSpec((None, local_kv, shard_len, head_size), lambda r, lens: (r, 0, 0, 0)),
            pl.BlockSpec((None, local_kv, shard_len, head_size), lambda r, lens: (r, 0, 0, 0)),
            pl.BlockSpec((None, local_kv, DRAFT_PAD, head_size), lambda r, lens: (r, 0, 0, 0)),
            pl.BlockSpec((None, local_kv, DRAFT_PAD, head_size), lambda r, lens: (r, 0, 0, 0)),
            pl.BlockSpec((None, tree_len, DRAFT_PAD), lambda r, lens: (r, 0, 0)),
        ],
        out_specs=[
            pl.BlockSpec((None, tree_len, local_heads, head_size), lambda r, lens: (r, 0, 0, 0)),
            pl.BlockSpec((None, local_kv, tree_len * group, 128), lambda r, lens: (r, 0, 0, 0)),
            pl.BlockSpec((None, local_kv, tree_len * group, 128), lambda r, lens: (r, 0, 0, 0)),
        ],
    )
    flops = 4 * requests * tree_len * local_heads * (shard_len + DRAFT_PAD) * head_size
    return pl.pallas_call(
        kernel,
        grid_spec=grid_spec,
        out_shape=[
            jax.ShapeDtypeStruct(queries.shape, jnp.float32),
            stats,
            stats,
        ],
        compiler_params=pltpu.CompilerParams(
            dimension_semantics=("arbitrary",),
            vmem_limit_bytes=48 * 1024 * 1024,
        ),
        cost_estimate=pl.CostEstimate(
            flops=flops,
            transcendentals=requests * tree_len * local_heads * (shard_len + DRAFT_PAD),
            bytes_accessed=2 * cache_keys.size * 2 + queries.size * 2 + queries.size * 4,
        ),
    )(local_len, queries, cache_keys, cache_values, draft_k, draft_v, draft_mask)


def local(
    queries, cache_keys, cache_values, lengths, parents, draft_keys, draft_values, out_weight
):
    requests, tree_len, local_heads, head_size = queries.shape
    shard_len = cache_keys.shape[1]
    local_kv = cache_keys.shape[2]
    group = local_heads // local_kv
    draft_len = draft_keys.shape[1]
    seq_size = lax.axis_size("seq")
    seq_index = lax.axis_index("seq")
    tree_mask = ancestry(parents)
    local_len = jnp.clip(lengths - seq_index * shard_len, 0, shard_len).astype(jnp.int32)
    draft_mask = lax.dynamic_slice_in_dim(tree_mask, seq_index * draft_len, draft_len, 2)
    draft_mask = jnp.pad(
        draft_mask.astype(jnp.float32), ((0, 0), (0, 0), (0, DRAFT_PAD - draft_len))
    )
    pad = ((0, 0), (0, 0), (0, DRAFT_PAD - draft_len), (0, 0))
    draft_k = jnp.pad(jnp.transpose(draft_keys, (0, 2, 1, 3)), pad)
    draft_v = jnp.pad(jnp.transpose(draft_values, (0, 2, 1, 3)), pad)
    numerator, top, total = attend(
        local_len, queries, jnp.transpose(cache_keys, (0, 2, 1, 3)),
        jnp.transpose(cache_values, (0, 2, 1, 3)), draft_k, draft_v, draft_mask
    )

    def per_head(stat):
        stat = stat[..., 0].reshape(requests, local_kv, tree_len, group)
        return jnp.transpose(stat, (0, 2, 1, 3)).reshape(requests, tree_len, local_heads)

    seq_size = lax.axis_size("seq")
    rows = requests * tree_len
    top = per_head(top)
    total = per_head(total)
    stats = jnp.concatenate(
        [top, total, jnp.zeros((requests, tree_len, head_size - 2 * local_heads), jnp.float32)],
        axis=-1,
    )
    packed = jnp.concatenate([numerator, stats[:, :, None, :]], axis=2)
    packed = packed.reshape(seq_size, rows // seq_size, local_heads + 1, head_size)
    got = lax.all_to_all(packed, "seq", 0, 0, tiled=True)
    got_stats = got[:, :, local_heads, :]
    got_common = got_stats[..., :local_heads]
    got_total = got_stats[..., local_heads:2 * local_heads]
    peak = jnp.max(got_common, axis=0)
    scaling = jnp.exp(got_common - peak)
    summed_total = jnp.sum(got_total * scaling, axis=0)
    summed = jnp.sum(got[:, :, :local_heads, :] * scaling[..., None], axis=0)
    mine_attended = (summed / summed_total[..., None]).astype(jnp.bfloat16)
    attended = lax.all_gather(mine_attended, "seq", axis=0, tiled=True)
    attended = attended.reshape(requests * tree_len, local_heads * head_size)
    terms = jnp.dot(attended, out_weight, preferred_element_type=jnp.float32)
    return lax.psum_scatter(terms, "head", scatter_dimension=1, tiled=True).astype(jnp.bfloat16)


def solution(mesh):
    return jax.shard_map(
        local,
        mesh=mesh,
        in_specs=(
            P(None, None, "head", None),
            P(None, "seq", "head", None),
            P(None, "seq", "head", None),
            P(),
            P(),
            P(None, "seq", "head", None),
            P(None, "seq", "head", None),
            P("head", "seq"),
        ),
        out_specs=P(None, ("seq", "head")),
        check_vma=False,
    )
```

```python
import functools

import jax
import jax.numpy as jnp
from jax import lax
from jax.experimental import pallas as pl
from jax.experimental.pallas import tpu as pltpu
from jax.sharding import PartitionSpec as P

NEG_BIG = -1e30
DRAFT_PAD = 128
ROW_TOKENS = 8
COLUMNS = 256


def ancestry(parents):
    tree_len = parents.shape[1]
    columns = jnp.arange(tree_len, dtype=jnp.int32)
    linked = (parents[:, :, None] == columns[None, None, :]) | (
        columns[:, None] == columns[None, :]
    )[None, :, :]
    reach = linked.astype(jnp.float32)
    for step in range(tree_len.bit_length()):
        reach = jnp.minimum(
            jnp.einsum("rij,rjk->rik", reach, reach, precision=lax.Precision.HIGHEST), 1.0
        )
    return reach > 0.5


def attend_kernel(lens_ref, q_ref, k_ref, v_ref, dk_ref, dv_ref, dmask_ref,
                  num_ref, top_ref, tot_ref, *, group, local_kv):
    r = pl.program_id(0)
    length = lens_ref[r]
    head_size = q_ref.shape[-1]
    shard_len = k_ref.shape[1]
    scale_factor = head_size ** (-0.5)
    rows = ROW_TOKENS * group
    dims = (((1,), (1,)), ((), ()))
    steps = shard_len // COLUMNS

    for kv in range(local_kv):
        heads = pl.ds(kv * group, group)

        def chunk(i, carry, kv=kv, heads=heads):
            t0 = pl.multiple_of(i * ROW_TOKENS, ROW_TOKENS)
            q = q_ref[pl.ds(t0, ROW_TOKENS), heads, :].reshape(rows, head_size)

            def scores_at(c):
                c0 = pl.multiple_of(c * COLUMNS, COLUMNS)
                keys = k_ref[kv, pl.ds(c0, COLUMNS), :]
                block = lax.dot_general(q, keys, dims, preferred_element_type=jnp.float32)

                def masked(block):
                    column = c0 + lax.broadcasted_iota(jnp.int32, block.shape, 1)
                    return jnp.where(column < length, block, NEG_BIG)

                return lax.cond(c0 + COLUMNS <= length, lambda b: b, masked, block), c0

            draft_scores = lax.dot_general(q, dk_ref[kv], dims, preferred_element_type=jnp.float32)
            draft_keep = dmask_ref[pl.ds(t0, ROW_TOKENS)]
            draft_keep = jnp.broadcast_to(
                draft_keep[:, None, :], (ROW_TOKENS, group, DRAFT_PAD)
            ).reshape(rows, DRAFT_PAD)
            draft_scores = jnp.where(draft_keep > 0.5, draft_scores, NEG_BIG)

            def find_top(c, top):
                block, _ = scores_at(c)
                return jnp.maximum(top, jnp.max(block, axis=-1, keepdims=True))

            top = lax.fori_loop(
                0, steps, find_top, jnp.max(draft_scores, axis=-1, keepdims=True), unroll=True
            )
            safe_top = jnp.maximum(top, NEG_BIG * 0.1)

            def accumulate(c, acc):
                total, numerator = acc
                block, c0 = scores_at(c)
                weight = jnp.exp((block - safe_top) * scale_factor)
                values = v_ref[kv, pl.ds(c0, COLUMNS), :]
                return (
                    total + jnp.sum(weight, axis=-1, keepdims=True),
                    numerator + jnp.dot(
                        weight.astype(jnp.bfloat16), values, preferred_element_type=jnp.float32
                    ),
                )

            draft_weight = jnp.exp((draft_scores - safe_top) * scale_factor)
            start = (
                jnp.sum(draft_weight, axis=-1, keepdims=True),
                jnp.dot(
                    draft_weight.astype(jnp.bfloat16), dv_ref[kv],
                    preferred_element_type=jnp.float32,
                ),
            )
            total, numerator = lax.fori_loop(0, steps, accumulate, start, unroll=True)
            num_ref[pl.ds(t0, ROW_TOKENS), heads, :] = numerator.reshape(
                ROW_TOKENS, group, head_size
            )
            r0 = pl.multiple_of(i * rows, rows)
            top_ref[kv, pl.ds(r0, rows), :] = jnp.broadcast_to(safe_top * scale_factor, (rows, 128))
            tot_ref[kv, pl.ds(r0, rows), :] = jnp.broadcast_to(total, (rows, 128))
            return carry

        lax.fori_loop(0, q_ref.shape[0] // ROW_TOKENS, chunk, 0)


def attend(local_len, queries, cache_keys, cache_values, draft_k, draft_v, draft_mask):
    requests, tree_len, local_heads, head_size = queries.shape
    local_kv = cache_keys.shape[1]
    shard_len = cache_keys.shape[2]
    group = local_heads // local_kv
    kernel = functools.partial(attend_kernel, group=group, local_kv=local_kv)
    stats = jax.ShapeDtypeStruct((requests, local_kv, tree_len * group, 128), jnp.float32)
    grid_spec = pltpu.PrefetchScalarGridSpec(
        num_scalar_prefetch=1,
        grid=(requests,),
        in_specs=[
            pl.BlockSpec((None, tree_len, local_heads, head_size), lambda r, lens: (r, 0, 0, 0)),
            pl.BlockSpec((None, local_kv, shard_len, head_size), lambda r, lens: (r, 0, 0, 0)),
            pl.BlockSpec((None, local_kv, shard_len, head_size), lambda r, lens: (r, 0, 0, 0)),
            pl.BlockSpec((None, local_kv, DRAFT_PAD, head_size), lambda r, lens: (r, 0, 0, 0)),
            pl.BlockSpec((None, local_kv, DRAFT_PAD, head_size), lambda r, lens: (r, 0, 0, 0)),
            pl.BlockSpec((None, tree_len, DRAFT_PAD), lambda r, lens: (r, 0, 0)),
        ],
        out_specs=[
            pl.BlockSpec((None, tree_len, local_heads, head_size), lambda r, lens: (r, 0, 0, 0)),
            pl.BlockSpec((None, local_kv, tree_len * group, 128), lambda r, lens: (r, 0, 0, 0)),
            pl.BlockSpec((None, local_kv, tree_len * group, 128), lambda r, lens: (r, 0, 0, 0)),
        ],
    )
    flops = 4 * requests * tree_len * local_heads * (shard_len + DRAFT_PAD) * head_size
    return pl.pallas_call(
        kernel,
        grid_spec=grid_spec,
        out_shape=[
            jax.ShapeDtypeStruct(queries.shape, jnp.float32),
            stats,
            stats,
        ],
        compiler_params=pltpu.CompilerParams(
            dimension_semantics=("arbitrary",),
            vmem_limit_bytes=48 * 1024 * 1024,
        ),
        cost_estimate=pl.CostEstimate(
            flops=flops,
            transcendentals=requests * tree_len * local_heads * (shard_len + DRAFT_PAD),
            bytes_accessed=2 * cache_keys.size * 2 + queries.size * 2 + queries.size * 4,
        ),
    )(local_len, queries, cache_keys, cache_values, draft_k, draft_v, draft_mask)


def local(
    queries, cache_keys, cache_values, lengths, parents, draft_keys, draft_values, out_weight
):
    requests, tree_len, local_heads, head_size = queries.shape
    shard_len = cache_keys.shape[1]
    local_kv = cache_keys.shape[2]
    group = local_heads // local_kv
    draft_len = draft_keys.shape[1]
    seq_size = lax.axis_size("seq")
    seq_index = lax.axis_index("seq")
    tree_mask = ancestry(parents)
    local_len = jnp.clip(lengths - seq_index * shard_len, 0, shard_len).astype(jnp.int32)
    draft_mask = lax.dynamic_slice_in_dim(tree_mask, seq_index * draft_len, draft_len, 2)
    draft_mask = jnp.pad(
        draft_mask.astype(jnp.float32), ((0, 0), (0, 0), (0, DRAFT_PAD - draft_len))
    )
    pad = ((0, 0), (0, 0), (0, DRAFT_PAD - draft_len), (0, 0))
    draft_k = jnp.pad(jnp.transpose(draft_keys, (0, 2, 1, 3)), pad)
    draft_v = jnp.pad(jnp.transpose(draft_values, (0, 2, 1, 3)), pad)
    numerator, top, total = attend(
        local_len, queries, jnp.transpose(cache_keys, (0, 2, 1, 3)),
        jnp.transpose(cache_values, (0, 2, 1, 3)), draft_k, draft_v, draft_mask
    )

    def per_head(stat):
        stat = stat[..., 0].reshape(requests, local_kv, tree_len, group)
        return jnp.transpose(stat, (0, 2, 1, 3)).reshape(requests, tree_len, local_heads)

    seq_size = lax.axis_size("seq")
    rows = requests * tree_len
    top = per_head(top)
    total = per_head(total)
    stats = jnp.concatenate(
        [top, total, jnp.zeros((requests, tree_len, head_size - 2 * local_heads), jnp.float32)],
        axis=-1,
    )
    packed = jnp.concatenate([numerator, stats[:, :, None, :]], axis=2)
    packed = packed.reshape(seq_size, rows // seq_size, local_heads + 1, head_size)
    packed = packed.reshape(seq_size, rows // seq_size, local_heads + 1, head_size)

    def combine(stack):
        common = stack[:, :, local_heads, :local_heads]
        peak = jnp.max(common, axis=0)
        scaling = jnp.exp(common - peak)
        summed_total = jnp.sum(stack[:, :, local_heads, local_heads:2 * local_heads] * scaling,
                               axis=0)
        summed = jnp.sum(stack[:, :, :local_heads, :] * scaling[..., None], axis=0)
        stats = jnp.concatenate(
            [peak, summed_total,
             jnp.zeros(peak.shape[:-1] + (head_size - 2 * local_heads,), jnp.float32)],
            axis=-1,
        )
        return jnp.concatenate([summed, stats[:, None, :]], axis=1)

    inner = 4 if seq_size % 4 == 0 else seq_size
    outer = seq_size // inner
    hi, lo = seq_index // inner, seq_index % inner
    grouped = packed.reshape(outer, inner, rows // seq_size, local_heads + 1, head_size)
    stage = [lax.dynamic_index_in_dim(grouped, lo, 1, keepdims=False)]
    for shift in range(1, inner):
        pairs = [(h * inner + l, h * inner + (l + shift) % inner)
                 for h in range(outer) for l in range(inner)]
        target = (lo + shift) % inner
        stage.append(lax.ppermute(
            lax.dynamic_index_in_dim(grouped, target, 1, keepdims=False), "seq", pairs))
    partial = jnp.stack(
        [combine(jnp.stack([piece[h] for piece in stage], axis=0)) for h in range(outer)], axis=0
    )
    final = [lax.dynamic_index_in_dim(partial, hi, 0, keepdims=False)]
    for shift in range(1, outer):
        pairs = [(h * inner + l, ((h + shift) % outer) * inner + l)
                 for h in range(outer) for l in range(inner)]
        target = (hi + shift) % outer
        final.append(lax.ppermute(
            lax.dynamic_index_in_dim(partial, target, 0, keepdims=False), "seq", pairs))
    mine = combine(jnp.stack(final, axis=0))
    summed = mine[:, :local_heads, :]
    summed_total = mine[:, local_heads, local_heads:2 * local_heads]
    mine_attended = (summed / summed_total[..., None]).astype(jnp.bfloat16)
    attended = lax.all_gather(mine_attended, "seq", axis=0, tiled=True)
    attended = attended.reshape(requests * tree_len, local_heads * head_size)
    terms = jnp.dot(attended, out_weight, preferred_element_type=jnp.float32)
    return lax.psum_scatter(terms, "head", scatter_dimension=1, tiled=True).astype(jnp.bfloat16)


def solution(mesh):
    return jax.shard_map(
        local,
        mesh=mesh,
        in_specs=(
            P(None, None, "head", None),
            P(None, "seq", "head", None),
            P(None, "seq", "head", None),
            P(),
            P(),
            P(None, "seq", "head", None),
            P(None, "seq", "head", None),
            P("head", "seq"),
        ),
        out_specs=P(None, ("seq", "head")),
        check_vma=False,
    )
```

```python
import functools

import jax
import jax.numpy as jnp
from jax import lax
from jax.experimental import pallas as pl
from jax.experimental.pallas import tpu as pltpu
from jax.sharding import PartitionSpec as P

NEG_BIG = -1e30
DRAFT_PAD = 128
ROW_TOKENS = 8
COLUMNS = 256


def ancestry(parents):
    tree_len = parents.shape[1]
    columns = jnp.arange(tree_len, dtype=jnp.int32)
    linked = (parents[:, :, None] == columns[None, None, :]) | (
        columns[:, None] == columns[None, :]
    )[None, :, :]
    reach = linked.astype(jnp.float32)
    for step in range(tree_len.bit_length()):
        reach = jnp.minimum(
            jnp.einsum("rij,rjk->rik", reach, reach, precision=lax.Precision.HIGHEST), 1.0
        )
    return reach > 0.5


def attend_kernel(lens_ref, q_ref, k_ref, v_ref, dk_ref, dv_ref, dmask_ref,
                  num_ref, top_ref, tot_ref, *, group, local_kv):
    r = pl.program_id(0)
    length = lens_ref[r]
    head_size = q_ref.shape[-1]
    shard_len = k_ref.shape[1]
    scale_factor = head_size ** (-0.5)
    rows = ROW_TOKENS * group
    dims = (((1,), (1,)), ((), ()))
    steps = shard_len // COLUMNS

    for kv in range(local_kv):
        heads = pl.ds(kv * group, group)

        def chunk(i, carry, kv=kv, heads=heads):
            t0 = pl.multiple_of(i * ROW_TOKENS, ROW_TOKENS)
            q = q_ref[pl.ds(t0, ROW_TOKENS), heads, :].reshape(rows, head_size)

            def scores_at(c):
                c0 = pl.multiple_of(c * COLUMNS, COLUMNS)
                keys = k_ref[kv, pl.ds(c0, COLUMNS), :]
                block = lax.dot_general(q, keys, dims, preferred_element_type=jnp.float32)

                def masked(block):
                    column = c0 + lax.broadcasted_iota(jnp.int32, block.shape, 1)
                    return jnp.where(column < length, block, NEG_BIG)

                return lax.cond(c0 + COLUMNS <= length, lambda b: b, masked, block), c0

            draft_scores = lax.dot_general(q, dk_ref[kv], dims, preferred_element_type=jnp.float32)
            draft_keep = dmask_ref[pl.ds(t0, ROW_TOKENS)]
            draft_keep = jnp.broadcast_to(
                draft_keep[:, None, :], (ROW_TOKENS, group, DRAFT_PAD)
            ).reshape(rows, DRAFT_PAD)
            draft_scores = jnp.where(draft_keep > 0.5, draft_scores, NEG_BIG)

            def find_top(c, top):
                block, _ = scores_at(c)
                return jnp.maximum(top, jnp.max(block, axis=-1, keepdims=True))

            top = lax.fori_loop(
                0, steps, find_top, jnp.max(draft_scores, axis=-1, keepdims=True), unroll=True
            )
            safe_top = jnp.maximum(top, NEG_BIG * 0.1)

            def accumulate(c, acc):
                total, numerator = acc
                block, c0 = scores_at(c)
                weight = jnp.exp((block - safe_top) * scale_factor)
                values = v_ref[kv, pl.ds(c0, COLUMNS), :]
                return (
                    total + jnp.sum(weight, axis=-1, keepdims=True),
                    numerator + jnp.dot(
                        weight.astype(jnp.bfloat16), values, preferred_element_type=jnp.float32
                    ),
                )

            draft_weight = jnp.exp((draft_scores - safe_top) * scale_factor)
            start = (
                jnp.sum(draft_weight, axis=-1, keepdims=True),
                jnp.dot(
                    draft_weight.astype(jnp.bfloat16), dv_ref[kv],
                    preferred_element_type=jnp.float32,
                ),
            )
            total, numerator = lax.fori_loop(0, steps, accumulate, start, unroll=True)
            num_ref[pl.ds(t0, ROW_TOKENS), heads, :] = numerator.reshape(
                ROW_TOKENS, group, head_size
            )
            r0 = pl.multiple_of(i * rows, rows)
            top_ref[kv, pl.ds(r0, rows), :] = jnp.broadcast_to(safe_top * scale_factor, (rows, 128))
            tot_ref[kv, pl.ds(r0, rows), :] = jnp.broadcast_to(total, (rows, 128))
            return carry

        lax.fori_loop(0, q_ref.shape[0] // ROW_TOKENS, chunk, 0)


def attend(local_len, queries, cache_keys, cache_values, draft_k, draft_v, draft_mask):
    requests, tree_len, local_heads, head_size = queries.shape
    local_kv = cache_keys.shape[1]
    shard_len = cache_keys.shape[2]
    group = local_heads // local_kv
    kernel = functools.partial(attend_kernel, group=group, local_kv=local_kv)
    stats = jax.ShapeDtypeStruct((requests, local_kv, tree_len * group, 128), jnp.float32)
    grid_spec = pltpu.PrefetchScalarGridSpec(
        num_scalar_prefetch=1,
        grid=(requests,),
        in_specs=[
            pl.BlockSpec((None, tree_len, local_heads, head_size), lambda r, lens: (r, 0, 0, 0)),
            pl.BlockSpec((None, local_kv, shard_len, head_size), lambda r, lens: (r, 0, 0, 0)),
            pl.BlockSpec((None, local_kv, shard_len, head_size), lambda r, lens: (r, 0, 0, 0)),
            pl.BlockSpec((None, local_kv, DRAFT_PAD, head_size), lambda r, lens: (r, 0, 0, 0)),
            pl.BlockSpec((None, local_kv, DRAFT_PAD, head_size), lambda r, lens: (r, 0, 0, 0)),
            pl.BlockSpec((None, tree_len, DRAFT_PAD), lambda r, lens: (r, 0, 0)),
        ],
        out_specs=[
            pl.BlockSpec((None, tree_len, local_heads, head_size), lambda r, lens: (r, 0, 0, 0)),
            pl.BlockSpec((None, local_kv, tree_len * group, 128), lambda r, lens: (r, 0, 0, 0)),
            pl.BlockSpec((None, local_kv, tree_len * group, 128), lambda r, lens: (r, 0, 0, 0)),
        ],
    )
    flops = 4 * requests * tree_len * local_heads * (shard_len + DRAFT_PAD) * head_size
    return pl.pallas_call(
        kernel,
        grid_spec=grid_spec,
        out_shape=[
            jax.ShapeDtypeStruct(queries.shape, jnp.float32),
            stats,
            stats,
        ],
        compiler_params=pltpu.CompilerParams(
            dimension_semantics=("arbitrary",),
            vmem_limit_bytes=48 * 1024 * 1024,
        ),
        cost_estimate=pl.CostEstimate(
            flops=flops,
            transcendentals=requests * tree_len * local_heads * (shard_len + DRAFT_PAD),
            bytes_accessed=2 * cache_keys.size * 2 + queries.size * 2 + queries.size * 4,
        ),
    )(local_len, queries, cache_keys, cache_values, draft_k, draft_v, draft_mask)


def local(
    queries, cache_keys, cache_values, lengths, parents, draft_keys, draft_values, out_weight
):
    requests, tree_len, local_heads, head_size = queries.shape
    shard_len = cache_keys.shape[1]
    local_kv = cache_keys.shape[2]
    group = local_heads // local_kv
    draft_len = draft_keys.shape[1]
    seq_size = lax.axis_size("seq")
    seq_index = lax.axis_index("seq")
    tree_mask = ancestry(parents)
    local_len = jnp.clip(lengths - seq_index * shard_len, 0, shard_len).astype(jnp.int32)
    draft_mask = lax.dynamic_slice_in_dim(tree_mask, seq_index * draft_len, draft_len, 2)
    draft_mask = jnp.pad(
        draft_mask.astype(jnp.float32), ((0, 0), (0, 0), (0, DRAFT_PAD - draft_len))
    )
    pad = ((0, 0), (0, 0), (0, DRAFT_PAD - draft_len), (0, 0))
    draft_k = jnp.pad(jnp.transpose(draft_keys, (0, 2, 1, 3)), pad)
    draft_v = jnp.pad(jnp.transpose(draft_values, (0, 2, 1, 3)), pad)
    numerator, top, total = attend(
        local_len, queries, jnp.transpose(cache_keys, (0, 2, 1, 3)),
        jnp.transpose(cache_values, (0, 2, 1, 3)), draft_k, draft_v, draft_mask
    )

    def per_head(stat):
        stat = stat[..., 0].reshape(requests, local_kv, tree_len, group)
        return jnp.transpose(stat, (0, 2, 1, 3)).reshape(requests, tree_len, local_heads)

    seq_size = lax.axis_size("seq")
    rows = requests * tree_len
    top = per_head(top)
    total = per_head(total)
    stats = jnp.concatenate(
        [top, total, jnp.zeros((requests, tree_len, head_size - 2 * local_heads), jnp.float32)],
        axis=-1,
    )
    packed = jnp.concatenate([numerator, stats[:, :, None, :]], axis=2)
    packed = packed.reshape(seq_size, rows // seq_size, local_heads + 1, head_size)
    packed = packed.reshape(seq_size, rows // seq_size, local_heads + 1, head_size)

    def combine(stack):
        common = stack[:, :, local_heads, :local_heads]
        peak = jnp.max(common, axis=0)
        scaling = jnp.exp(common - peak)
        summed_total = jnp.sum(stack[:, :, local_heads, local_heads:2 * local_heads] * scaling,
                               axis=0)
        summed = jnp.sum(stack[:, :, :local_heads, :] * scaling[..., None], axis=0)
        stats = jnp.concatenate(
            [peak, summed_total,
             jnp.zeros(peak.shape[:-1] + (head_size - 2 * local_heads,), jnp.float32)],
            axis=-1,
        )
        return jnp.concatenate([summed, stats[:, None, :]], axis=1)

    inner = 4 if seq_size % 4 == 0 else seq_size
    outer = seq_size // inner
    hi, lo = seq_index // inner, seq_index % inner
    grouped = packed.reshape(outer, inner, rows // seq_size, local_heads + 1, head_size)
    stage = [lax.dynamic_index_in_dim(grouped, lo, 1, keepdims=False)]
    for shift in range(1, inner):
        pairs = [(h * inner + l, h * inner + (l + shift) % inner)
                 for h in range(outer) for l in range(inner)]
        target = (lo + shift) % inner
        stage.append(lax.ppermute(
            lax.dynamic_index_in_dim(grouped, target, 1, keepdims=False), "seq", pairs))
    partial = jnp.stack(
        [combine(jnp.stack([piece[h] for piece in stage], axis=0)) for h in range(outer)], axis=0
    )
    final = [lax.dynamic_index_in_dim(partial, hi, 0, keepdims=False)]
    for shift in range(1, outer):
        pairs = [(h * inner + l, ((h + shift) % outer) * inner + l)
                 for h in range(outer) for l in range(inner)]
        target = (hi + shift) % outer
        final.append(lax.ppermute(
            lax.dynamic_index_in_dim(partial, target, 0, keepdims=False), "seq", pairs))
    mine = combine(jnp.stack(final, axis=0))
    summed = mine[:, :local_heads, :]
    summed_total = mine[:, local_heads, local_heads:2 * local_heads]
    mine_attended = (summed / summed_total[..., None]).astype(jnp.bfloat16)
    across = [mine_attended]
    for shift in range(1, outer):
        pairs = [(h * inner + l, ((h + shift) % outer) * inner + l)
                 for h in range(outer) for l in range(inner)]
        across.append(lax.ppermute(mine_attended, "seq", pairs))
    by_outer = jnp.zeros((outer,) + mine_attended.shape, jnp.bfloat16)
    for shift, piece in enumerate(across):
        by_outer = lax.dynamic_update_index_in_dim(by_outer, piece, (hi - shift) % outer, 0)
    gathered = jnp.zeros((outer, inner) + mine_attended.shape, jnp.bfloat16)
    gathered = lax.dynamic_update_index_in_dim(gathered, by_outer, lo, 1)
    for shift in range(1, inner):
        pairs = [(h * inner + l, h * inner + (l + shift) % inner)
                 for h in range(outer) for l in range(inner)]
        got_piece = lax.ppermute(by_outer, "seq", pairs)
        gathered = lax.dynamic_update_index_in_dim(gathered, got_piece, (lo - shift) % inner, 1)
    attended = gathered
    attended = attended.reshape(requests * tree_len, local_heads * head_size)
    terms = jnp.dot(attended, out_weight, preferred_element_type=jnp.float32)
    return lax.psum_scatter(terms, "head", scatter_dimension=1, tiled=True).astype(jnp.bfloat16)


def solution(mesh):
    return jax.shard_map(
        local,
        mesh=mesh,
        in_specs=(
            P(None, None, "head", None),
            P(None, "seq", "head", None),
            P(None, "seq", "head", None),
            P(),
            P(),
            P(None, "seq", "head", None),
            P(None, "seq", "head", None),
            P("head", "seq"),
        ),
        out_specs=P(None, ("seq", "head")),
        check_vma=False,
    )
```

```python
import functools

import jax
import jax.numpy as jnp
from jax import lax
from jax.experimental import pallas as pl
from jax.experimental.pallas import tpu as pltpu
from jax.sharding import PartitionSpec as P

NEG_BIG = -1e30
DRAFT_PAD = 128
ROW_TOKENS = 8
COLUMNS = 256


def ancestry(parents):
    tree_len = parents.shape[1]
    columns = jnp.arange(tree_len, dtype=jnp.int32)
    linked = (parents[:, :, None] == columns[None, None, :]) | (
        columns[:, None] == columns[None, :]
    )[None, :, :]
    reach = linked.astype(jnp.float32)
    for step in range(tree_len.bit_length()):
        reach = jnp.minimum(
            jnp.einsum("rij,rjk->rik", reach, reach, precision=lax.Precision.HIGHEST), 1.0
        )
    return reach > 0.5


def attend_kernel(lens_ref, q_ref, k_ref, v_ref, dk_ref, dv_ref, dmask_ref,
                  num_ref, top_ref, tot_ref, *, group, local_kv):
    r = pl.program_id(0)
    length = lens_ref[r]
    head_size = q_ref.shape[-1]
    shard_len = k_ref.shape[1]
    scale_factor = head_size ** (-0.5)
    rows = ROW_TOKENS * group
    dims = (((1,), (1,)), ((), ()))
    steps = shard_len // COLUMNS

    for kv in range(local_kv):
        heads = pl.ds(kv * group, group)

        def chunk(i, carry, kv=kv, heads=heads):
            t0 = pl.multiple_of(i * ROW_TOKENS, ROW_TOKENS)
            q = q_ref[pl.ds(t0, ROW_TOKENS), heads, :].reshape(rows, head_size)

            def scores_at(c):
                c0 = pl.multiple_of(c * COLUMNS, COLUMNS)
                keys = k_ref[kv, pl.ds(c0, COLUMNS), :]
                block = lax.dot_general(q, keys, dims, preferred_element_type=jnp.float32)

                def masked(block):
                    column = c0 + lax.broadcasted_iota(jnp.int32, block.shape, 1)
                    return jnp.where(column < length, block, NEG_BIG)

                return lax.cond(c0 + COLUMNS <= length, lambda b: b, masked, block), c0

            draft_scores = lax.dot_general(q, dk_ref[kv], dims, preferred_element_type=jnp.float32)
            draft_keep = dmask_ref[pl.ds(t0, ROW_TOKENS)]
            draft_keep = jnp.broadcast_to(
                draft_keep[:, None, :], (ROW_TOKENS, group, DRAFT_PAD)
            ).reshape(rows, DRAFT_PAD)
            draft_scores = jnp.where(draft_keep > 0.5, draft_scores, NEG_BIG)

            def find_top(c, top):
                block, _ = scores_at(c)
                return jnp.maximum(top, jnp.max(block, axis=-1, keepdims=True))

            top = lax.fori_loop(
                0, steps, find_top, jnp.max(draft_scores, axis=-1, keepdims=True), unroll=True
            )
            safe_top = jnp.maximum(top, NEG_BIG * 0.1)

            def accumulate(c, acc):
                total, numerator = acc
                block, c0 = scores_at(c)
                weight = jnp.exp((block - safe_top) * scale_factor)
                values = v_ref[kv, pl.ds(c0, COLUMNS), :]
                return (
                    total + jnp.sum(weight, axis=-1, keepdims=True),
                    numerator + jnp.dot(
                        weight.astype(jnp.bfloat16), values, preferred_element_type=jnp.float32
                    ),
                )

            draft_weight = jnp.exp((draft_scores - safe_top) * scale_factor)
            start = (
                jnp.sum(draft_weight, axis=-1, keepdims=True),
                jnp.dot(
                    draft_weight.astype(jnp.bfloat16), dv_ref[kv],
                    preferred_element_type=jnp.float32,
                ),
            )
            total, numerator = lax.fori_loop(0, steps, accumulate, start, unroll=True)
            num_ref[pl.ds(t0, ROW_TOKENS), heads, :] = numerator.reshape(
                ROW_TOKENS, group, head_size
            )
            r0 = pl.multiple_of(i * rows, rows)
            top_ref[kv, pl.ds(r0, rows), :] = jnp.broadcast_to(safe_top * scale_factor, (rows, 128))
            tot_ref[kv, pl.ds(r0, rows), :] = jnp.broadcast_to(total, (rows, 128))
            return carry

        lax.fori_loop(0, q_ref.shape[0] // ROW_TOKENS, chunk, 0)


def attend(local_len, queries, cache_keys, cache_values, draft_k, draft_v, draft_mask):
    requests, tree_len, local_heads, head_size = queries.shape
    local_kv = cache_keys.shape[1]
    shard_len = cache_keys.shape[2]
    group = local_heads // local_kv
    kernel = functools.partial(attend_kernel, group=group, local_kv=local_kv)
    stats = jax.ShapeDtypeStruct((requests, local_kv, tree_len * group, 128), jnp.float32)
    grid_spec = pltpu.PrefetchScalarGridSpec(
        num_scalar_prefetch=1,
        grid=(requests,),
        in_specs=[
            pl.BlockSpec((None, tree_len, local_heads, head_size), lambda r, lens: (r, 0, 0, 0)),
            pl.BlockSpec((None, local_kv, shard_len, head_size), lambda r, lens: (r, 0, 0, 0)),
            pl.BlockSpec((None, local_kv, shard_len, head_size), lambda r, lens: (r, 0, 0, 0)),
            pl.BlockSpec((None, local_kv, DRAFT_PAD, head_size), lambda r, lens: (r, 0, 0, 0)),
            pl.BlockSpec((None, local_kv, DRAFT_PAD, head_size), lambda r, lens: (r, 0, 0, 0)),
            pl.BlockSpec((None, tree_len, DRAFT_PAD), lambda r, lens: (r, 0, 0)),
        ],
        out_specs=[
            pl.BlockSpec((None, tree_len, local_heads, head_size), lambda r, lens: (r, 0, 0, 0)),
            pl.BlockSpec((None, local_kv, tree_len * group, 128), lambda r, lens: (r, 0, 0, 0)),
            pl.BlockSpec((None, local_kv, tree_len * group, 128), lambda r, lens: (r, 0, 0, 0)),
        ],
    )
    flops = 4 * requests * tree_len * local_heads * (shard_len + DRAFT_PAD) * head_size
    return pl.pallas_call(
        kernel,
        grid_spec=grid_spec,
        out_shape=[
            jax.ShapeDtypeStruct(queries.shape, jnp.float32),
            stats,
            stats,
        ],
        compiler_params=pltpu.CompilerParams(
            dimension_semantics=("arbitrary",),
            vmem_limit_bytes=48 * 1024 * 1024,
        ),
        cost_estimate=pl.CostEstimate(
            flops=flops,
            transcendentals=requests * tree_len * local_heads * (shard_len + DRAFT_PAD),
            bytes_accessed=2 * cache_keys.size * 2 + queries.size * 2 + queries.size * 4,
        ),
    )(local_len, queries, cache_keys, cache_values, draft_k, draft_v, draft_mask)


def local(
    queries, cache_keys, cache_values, lengths, parents, draft_keys, draft_values, out_weight
):
    requests, tree_len, local_heads, head_size = queries.shape
    shard_len = cache_keys.shape[1]
    local_kv = cache_keys.shape[2]
    group = local_heads // local_kv
    draft_len = draft_keys.shape[1]
    seq_size = lax.axis_size("seq")
    seq_index = lax.axis_index("seq")
    tree_mask = ancestry(parents)
    local_len = jnp.clip(lengths - seq_index * shard_len, 0, shard_len).astype(jnp.int32)
    draft_mask = lax.dynamic_slice_in_dim(tree_mask, seq_index * draft_len, draft_len, 2)
    draft_mask = jnp.pad(
        draft_mask.astype(jnp.float32), ((0, 0), (0, 0), (0, DRAFT_PAD - draft_len))
    )
    pad = ((0, 0), (0, 0), (0, DRAFT_PAD - draft_len), (0, 0))
    draft_k = jnp.pad(jnp.transpose(draft_keys, (0, 2, 1, 3)), pad)
    draft_v = jnp.pad(jnp.transpose(draft_values, (0, 2, 1, 3)), pad)
    numerator, top, total = attend(
        local_len, queries, jnp.transpose(cache_keys, (0, 2, 1, 3)),
        jnp.transpose(cache_values, (0, 2, 1, 3)), draft_k, draft_v, draft_mask
    )

    def per_head(stat):
        stat = stat[..., 0].reshape(requests, local_kv, tree_len, group)
        return jnp.transpose(stat, (0, 2, 1, 3)).reshape(requests, tree_len, local_heads)

    seq_size = lax.axis_size("seq")
    rows = requests * tree_len
    top = per_head(top)
    total = per_head(total)
    stats = jnp.concatenate(
        [top, total, jnp.zeros((requests, tree_len, head_size - 2 * local_heads), jnp.float32)],
        axis=-1,
    )
    packed = jnp.concatenate([numerator, stats[:, :, None, :]], axis=2)
    packed = packed.reshape(seq_size, rows // seq_size, local_heads + 1, head_size)
    packed = packed.reshape(seq_size, rows // seq_size, local_heads + 1, head_size)

    def combine(stack):
        common = stack[:, :, local_heads, :local_heads]
        peak = jnp.max(common, axis=0)
        scaling = jnp.exp(common - peak)
        summed_total = jnp.sum(stack[:, :, local_heads, local_heads:2 * local_heads] * scaling,
                               axis=0)
        summed = jnp.sum(stack[:, :, :local_heads, :] * scaling[..., None], axis=0)
        stats = jnp.concatenate(
            [peak, summed_total,
             jnp.zeros(peak.shape[:-1] + (head_size - 2 * local_heads,), jnp.float32)],
            axis=-1,
        )
        return jnp.concatenate([summed, stats[:, None, :]], axis=1)

    inner = 4 if seq_size % 4 == 0 else seq_size
    outer = seq_size // inner
    hi, lo = seq_index // inner, seq_index % inner
    grouped = packed.reshape(outer, inner, rows // seq_size, local_heads + 1, head_size)
    stage = [lax.dynamic_index_in_dim(grouped, lo, 1, keepdims=False)]
    for shift in range(1, inner):
        pairs = [(h * inner + l, h * inner + (l + shift) % inner)
                 for h in range(outer) for l in range(inner)]
        target = (lo + shift) % inner
        stage.append(lax.ppermute(
            lax.dynamic_index_in_dim(grouped, target, 1, keepdims=False), "seq", pairs))
    partial = jnp.stack(
        [combine(jnp.stack([piece[h] for piece in stage], axis=0)) for h in range(outer)], axis=0
    )
    final = [lax.dynamic_index_in_dim(partial, hi, 0, keepdims=False)]
    for shift in range(1, outer):
        pairs = [(h * inner + l, ((h + shift) % outer) * inner + l)
                 for h in range(outer) for l in range(inner)]
        target = (hi + shift) % outer
        final.append(lax.ppermute(
            lax.dynamic_index_in_dim(partial, target, 0, keepdims=False), "seq", pairs))
    mine = combine(jnp.stack(final, axis=0))
    summed = mine[:, :local_heads, :]
    summed_total = mine[:, local_heads, local_heads:2 * local_heads]
    mine_attended = (summed / summed_total[..., None]).astype(jnp.bfloat16)
    across = [mine_attended]
    for shift in range(1, outer):
        pairs = [(h * inner + l, ((h + shift) % outer) * inner + l)
                 for h in range(outer) for l in range(inner)]
        across.append(lax.ppermute(mine_attended, "seq", pairs))
    by_outer = jnp.zeros((outer,) + mine_attended.shape, jnp.bfloat16)
    for shift, piece in enumerate(across):
        by_outer = lax.dynamic_update_index_in_dim(by_outer, piece, (hi - shift) % outer, 0)
    gathered = jnp.zeros((outer, inner) + mine_attended.shape, jnp.bfloat16)
    gathered = lax.dynamic_update_index_in_dim(gathered, by_outer, lo, 1)
    for shift in range(1, inner):
        pairs = [(h * inner + l, h * inner + (l + shift) % inner)
                 for h in range(outer) for l in range(inner)]
        got_piece = lax.ppermute(by_outer, "seq", pairs)
        gathered = lax.dynamic_update_index_in_dim(gathered, got_piece, (lo - shift) % inner, 1)
    attended = gathered
    attended = attended.reshape(requests * tree_len, local_heads * head_size)
    terms = jnp.dot(attended, out_weight, preferred_element_type=jnp.float32)
    head_count = lax.axis_size("head")
    if head_count & (head_count - 1):
        return lax.psum_scatter(terms, "head", scatter_dimension=1, tiled=True).astype(
            jnp.bfloat16
        )
    head_index = lax.axis_index("head")
    width = terms.shape[1] // head_count
    kept = terms.reshape(rows, head_count, width)
    bit = 1
    while bit < head_count:
        mine_bit = (head_index // bit) % 2
        halves = kept.reshape(rows, kept.shape[1] // 2, 2, width)
        keep = lax.dynamic_index_in_dim(halves, mine_bit, 2, keepdims=False)
        send = lax.dynamic_index_in_dim(halves, 1 - mine_bit, 2, keepdims=False)
        kept = keep + lax.ppermute(send, "head", [(i, i ^ bit) for i in range(head_count)])
        bit *= 2
    return kept.reshape(rows, width).astype(jnp.bfloat16)


def solution(mesh):
    return jax.shard_map(
        local,
        mesh=mesh,
        in_specs=(
            P(None, None, "head", None),
            P(None, "seq", "head", None),
            P(None, "seq", "head", None),
            P(),
            P(),
            P(None, "seq", "head", None),
            P(None, "seq", "head", None),
            P("head", "seq"),
        ),
        out_specs=P(None, ("seq", "head")),
        check_vma=False,
    )
```

```python
import functools

import jax
import jax.numpy as jnp
from jax import lax
from jax.experimental import pallas as pl
from jax.experimental.pallas import tpu as pltpu
from jax.sharding import PartitionSpec as P

NEG_BIG = -1e30
DRAFT_PAD = 128
ROW_TOKENS = 8
COLUMNS = 256


def ancestry(parents):
    tree_len = parents.shape[1]
    columns = jnp.arange(tree_len, dtype=jnp.int32)
    linked = (parents[:, :, None] == columns[None, None, :]) | (
        columns[:, None] == columns[None, :]
    )[None, :, :]
    reach = linked.astype(jnp.float32)
    for step in range(tree_len.bit_length()):
        reach = jnp.minimum(
            jnp.einsum("rij,rjk->rik", reach, reach, precision=lax.Precision.HIGHEST), 1.0
        )
    return reach > 0.5


def attend_kernel(lens_ref, q_ref, k_ref, v_ref, dk_ref, dv_ref, dmask_ref,
                  num_ref, top_ref, tot_ref, *, group, local_kv):
    r = pl.program_id(0)
    length = lens_ref[r]
    head_size = q_ref.shape[-1]
    shard_len = k_ref.shape[1]
    scale_factor = head_size ** (-0.5)
    rows = ROW_TOKENS * group
    dims = (((1,), (1,)), ((), ()))
    steps = shard_len // COLUMNS

    for kv in range(local_kv):
        heads = pl.ds(kv * group, group)

        def chunk(i, carry, kv=kv, heads=heads):
            t0 = pl.multiple_of(i * ROW_TOKENS, ROW_TOKENS)
            q = q_ref[pl.ds(t0, ROW_TOKENS), heads, :].reshape(rows, head_size)

            def scores_at(c):
                c0 = pl.multiple_of(c * COLUMNS, COLUMNS)
                keys = k_ref[kv, pl.ds(c0, COLUMNS), :]
                block = lax.dot_general(q, keys, dims, preferred_element_type=jnp.float32)

                def masked(block):
                    column = c0 + lax.broadcasted_iota(jnp.int32, block.shape, 1)
                    return jnp.where(column < length, block, NEG_BIG)

                return lax.cond(c0 + COLUMNS <= length, lambda b: b, masked, block), c0

            draft_scores = lax.dot_general(q, dk_ref[kv], dims, preferred_element_type=jnp.float32)
            draft_keep = dmask_ref[pl.ds(t0, ROW_TOKENS)]
            draft_keep = jnp.broadcast_to(
                draft_keep[:, None, :], (ROW_TOKENS, group, DRAFT_PAD)
            ).reshape(rows, DRAFT_PAD)
            draft_scores = jnp.where(draft_keep > 0.5, draft_scores, NEG_BIG)

            def find_top(c, top):
                block, _ = scores_at(c)
                return jnp.maximum(top, jnp.max(block, axis=-1, keepdims=True))

            top = lax.fori_loop(
                0, steps, find_top, jnp.max(draft_scores, axis=-1, keepdims=True), unroll=True
            )
            safe_top = jnp.maximum(top, NEG_BIG * 0.1)

            def accumulate(c, acc):
                total, numerator = acc
                block, c0 = scores_at(c)
                weight = jnp.exp((block - safe_top) * scale_factor)
                values = v_ref[kv, pl.ds(c0, COLUMNS), :]
                return (
                    total + jnp.sum(weight, axis=-1, keepdims=True),
                    numerator + jnp.dot(
                        weight.astype(jnp.bfloat16), values, preferred_element_type=jnp.float32
                    ),
                )

            draft_weight = jnp.exp((draft_scores - safe_top) * scale_factor)
            start = (
                jnp.sum(draft_weight, axis=-1, keepdims=True),
                jnp.dot(
                    draft_weight.astype(jnp.bfloat16), dv_ref[kv],
                    preferred_element_type=jnp.float32,
                ),
            )
            total, numerator = lax.fori_loop(0, steps, accumulate, start, unroll=True)
            num_ref[pl.ds(t0, ROW_TOKENS), heads, :] = numerator.reshape(
                ROW_TOKENS, group, head_size
            )
            r0 = pl.multiple_of(i * rows, rows)
            top_ref[kv, pl.ds(r0, rows), :] = jnp.broadcast_to(safe_top * scale_factor, (rows, 128))
            tot_ref[kv, pl.ds(r0, rows), :] = jnp.broadcast_to(total, (rows, 128))
            return carry

        lax.fori_loop(0, q_ref.shape[0] // ROW_TOKENS, chunk, 0)


def attend(local_len, queries, cache_keys, cache_values, draft_k, draft_v, draft_mask):
    requests, tree_len, local_heads, head_size = queries.shape
    local_kv = cache_keys.shape[1]
    shard_len = cache_keys.shape[2]
    group = local_heads // local_kv
    kernel = functools.partial(attend_kernel, group=group, local_kv=local_kv)
    stats = jax.ShapeDtypeStruct((requests, local_kv, tree_len * group, 128), jnp.float32)
    grid_spec = pltpu.PrefetchScalarGridSpec(
        num_scalar_prefetch=1,
        grid=(requests,),
        in_specs=[
            pl.BlockSpec((None, tree_len, local_heads, head_size), lambda r, lens: (r, 0, 0, 0)),
            pl.BlockSpec((None, local_kv, shard_len, head_size), lambda r, lens: (r, 0, 0, 0)),
            pl.BlockSpec((None, local_kv, shard_len, head_size), lambda r, lens: (r, 0, 0, 0)),
            pl.BlockSpec((None, local_kv, DRAFT_PAD, head_size), lambda r, lens: (r, 0, 0, 0)),
            pl.BlockSpec((None, local_kv, DRAFT_PAD, head_size), lambda r, lens: (r, 0, 0, 0)),
            pl.BlockSpec((None, tree_len, DRAFT_PAD), lambda r, lens: (r, 0, 0)),
        ],
        out_specs=[
            pl.BlockSpec((None, tree_len, local_heads, head_size), lambda r, lens: (r, 0, 0, 0)),
            pl.BlockSpec((None, local_kv, tree_len * group, 128), lambda r, lens: (r, 0, 0, 0)),
            pl.BlockSpec((None, local_kv, tree_len * group, 128), lambda r, lens: (r, 0, 0, 0)),
        ],
    )
    flops = 4 * requests * tree_len * local_heads * (shard_len + DRAFT_PAD) * head_size
    return pl.pallas_call(
        kernel,
        grid_spec=grid_spec,
        out_shape=[
            jax.ShapeDtypeStruct(queries.shape, jnp.float32),
            stats,
            stats,
        ],
        compiler_params=pltpu.CompilerParams(
            dimension_semantics=("arbitrary",),
            vmem_limit_bytes=48 * 1024 * 1024,
        ),
        cost_estimate=pl.CostEstimate(
            flops=flops,
            transcendentals=requests * tree_len * local_heads * (shard_len + DRAFT_PAD),
            bytes_accessed=2 * cache_keys.size * 2 + queries.size * 2 + queries.size * 4,
        ),
    )(local_len, queries, cache_keys, cache_values, draft_k, draft_v, draft_mask)


def local(
    queries, cache_keys, cache_values, lengths, parents, draft_keys, draft_values, out_weight
):
    requests, tree_len, local_heads, head_size = queries.shape
    shard_len = cache_keys.shape[1]
    local_kv = cache_keys.shape[2]
    group = local_heads // local_kv
    draft_len = draft_keys.shape[1]
    seq_size = lax.axis_size("seq")
    seq_index = lax.axis_index("seq")
    tree_mask = ancestry(parents)
    local_len = jnp.clip(lengths - seq_index * shard_len, 0, shard_len).astype(jnp.int32)
    draft_mask = lax.dynamic_slice_in_dim(tree_mask, seq_index * draft_len, draft_len, 2)
    draft_mask = jnp.pad(
        draft_mask.astype(jnp.float32), ((0, 0), (0, 0), (0, DRAFT_PAD - draft_len))
    )
    pad = ((0, 0), (0, 0), (0, DRAFT_PAD - draft_len), (0, 0))
    draft_k = jnp.pad(jnp.transpose(draft_keys, (0, 2, 1, 3)), pad)
    draft_v = jnp.pad(jnp.transpose(draft_values, (0, 2, 1, 3)), pad)
    numerator, top, total = attend(
        local_len, queries, jnp.transpose(cache_keys, (0, 2, 1, 3)),
        jnp.transpose(cache_values, (0, 2, 1, 3)), draft_k, draft_v, draft_mask
    )

    def per_head(stat):
        stat = stat[..., 0].reshape(requests, local_kv, tree_len, group)
        return jnp.transpose(stat, (0, 2, 1, 3)).reshape(requests, tree_len, local_heads)

    seq_size = lax.axis_size("seq")
    rows = requests * tree_len
    top = per_head(top)
    total = per_head(total)
    stats = jnp.concatenate(
        [top, total, jnp.zeros((requests, tree_len, head_size - 2 * local_heads), jnp.float32)],
        axis=-1,
    )
    packed = jnp.concatenate([numerator, stats[:, :, None, :]], axis=2)
    packed = packed.reshape(seq_size, rows // seq_size, local_heads + 1, head_size)
    packed = packed.reshape(seq_size, rows // seq_size, local_heads + 1, head_size)

    def combine(stack):
        common = stack[:, :, local_heads, :local_heads]
        peak = jnp.max(common, axis=0)
        scaling = jnp.exp(common - peak)
        summed_total = jnp.sum(stack[:, :, local_heads, local_heads:2 * local_heads] * scaling,
                               axis=0)
        summed = jnp.sum(stack[:, :, :local_heads, :] * scaling[..., None], axis=0)
        stats = jnp.concatenate(
            [peak, summed_total,
             jnp.zeros(peak.shape[:-1] + (head_size - 2 * local_heads,), jnp.float32)],
            axis=-1,
        )
        return jnp.concatenate([summed, stats[:, None, :]], axis=1)

    inner = 4 if seq_size % 4 == 0 else seq_size
    outer = seq_size // inner
    hi, lo = seq_index // inner, seq_index % inner
    grouped = packed.reshape(outer, inner, rows // seq_size, local_heads + 1, head_size)
    stage = [lax.dynamic_index_in_dim(grouped, lo, 1, keepdims=False)]
    for shift in range(1, inner):
        pairs = [(h * inner + l, h * inner + (l + shift) % inner)
                 for h in range(outer) for l in range(inner)]
        target = (lo + shift) % inner
        stage.append(lax.ppermute(
            lax.dynamic_index_in_dim(grouped, target, 1, keepdims=False), "seq", pairs))
    partial = jnp.stack(
        [combine(jnp.stack([piece[h] for piece in stage], axis=0)) for h in range(outer)], axis=0
    )
    final = [lax.dynamic_index_in_dim(partial, hi, 0, keepdims=False)]
    for shift in range(1, outer):
        pairs = [(h * inner + l, ((h + shift) % outer) * inner + l)
                 for h in range(outer) for l in range(inner)]
        target = (hi + shift) % outer
        final.append(lax.ppermute(
            lax.dynamic_index_in_dim(partial, target, 0, keepdims=False), "seq", pairs))
    mine = combine(jnp.stack(final, axis=0))
    summed = mine[:, :local_heads, :]
    summed_total = mine[:, local_heads, local_heads:2 * local_heads]
    mine_attended = (summed / summed_total[..., None]).astype(jnp.bfloat16)
    across = [mine_attended]
    for shift in range(1, outer):
        pairs = [(h * inner + l, ((h + shift) % outer) * inner + l)
                 for h in range(outer) for l in range(inner)]
        across.append(lax.ppermute(mine_attended, "seq", pairs))
    by_outer = jnp.zeros((outer,) + mine_attended.shape, jnp.bfloat16)
    for shift, piece in enumerate(across):
        by_outer = lax.dynamic_update_index_in_dim(by_outer, piece, (hi - shift) % outer, 0)
    gathered = jnp.zeros((outer, inner) + mine_attended.shape, jnp.bfloat16)
    gathered = lax.dynamic_update_index_in_dim(gathered, by_outer, lo, 1)
    for shift in range(1, inner):
        pairs = [(h * inner + l, h * inner + (l + shift) % inner)
                 for h in range(outer) for l in range(inner)]
        got_piece = lax.ppermute(by_outer, "seq", pairs)
        gathered = lax.dynamic_update_index_in_dim(gathered, got_piece, (lo - shift) % inner, 1)
    attended = gathered
    attended = attended.reshape(requests * tree_len, local_heads * head_size)
    terms = jnp.dot(attended, out_weight, preferred_element_type=jnp.float32)
    head_count = lax.axis_size("head")
    if head_count & (head_count - 1):
        return lax.psum_scatter(terms, "head", scatter_dimension=1, tiled=True).astype(
            jnp.bfloat16
        )
    head_index = lax.axis_index("head")
    width = terms.shape[1] // head_count
    kept = lax.optimization_barrier(terms).reshape(rows, head_count, width)
    bit = 1
    while bit < head_count:
        mine_bit = (head_index // bit) % 2
        halves = kept.reshape(rows, kept.shape[1] // 2, 2, width)
        keep = lax.dynamic_index_in_dim(halves, mine_bit, 2, keepdims=False)
        send = lax.dynamic_index_in_dim(halves, 1 - mine_bit, 2, keepdims=False)
        kept = keep + lax.ppermute(send, "head", [(i, i ^ bit) for i in range(head_count)])
        bit *= 2
    return kept.reshape(rows, width).astype(jnp.bfloat16)


def solution(mesh):
    return jax.shard_map(
        local,
        mesh=mesh,
        in_specs=(
            P(None, None, "head", None),
            P(None, "seq", "head", None),
            P(None, "seq", "head", None),
            P(),
            P(),
            P(None, "seq", "head", None),
            P(None, "seq", "head", None),
            P("head", "seq"),
        ),
        out_specs=P(None, ("seq", "head")),
        check_vma=False,
    )
```

```python
import functools

import jax
import jax.numpy as jnp
from jax import lax
from jax.experimental import pallas as pl
from jax.experimental.pallas import tpu as pltpu
from jax.sharding import PartitionSpec as P

NEG_BIG = -1e30
DRAFT_PAD = 128
ROW_TOKENS = 8
COLUMNS = 256


def ancestry(parents):
    tree_len = parents.shape[1]
    columns = jnp.arange(tree_len, dtype=jnp.int32)
    linked = (parents[:, :, None] == columns[None, None, :]) | (
        columns[:, None] == columns[None, :]
    )[None, :, :]
    reach = linked.astype(jnp.float32)
    for step in range(tree_len.bit_length()):
        reach = jnp.minimum(
            jnp.einsum("rij,rjk->rik", reach, reach, precision=lax.Precision.HIGHEST), 1.0
        )
    return reach > 0.5


def attend_kernel(lens_ref, q_ref, k_ref, v_ref, dk_ref, dv_ref, dmask_ref,
                  num_ref, top_ref, tot_ref, *, group, local_kv):
    r = pl.program_id(0)
    length = lens_ref[r]
    head_size = q_ref.shape[-1]
    shard_len = k_ref.shape[1]
    scale_factor = head_size ** (-0.5)
    rows = ROW_TOKENS * group
    dims = (((1,), (1,)), ((), ()))
    steps = shard_len // COLUMNS

    for kv in range(local_kv):
        heads = pl.ds(kv * group, group)

        def chunk(i, carry, kv=kv, heads=heads):
            t0 = pl.multiple_of(i * ROW_TOKENS, ROW_TOKENS)
            q = q_ref[pl.ds(t0, ROW_TOKENS), heads, :].reshape(rows, head_size)

            def scores_at(c):
                c0 = pl.multiple_of(c * COLUMNS, COLUMNS)
                keys = k_ref[kv, pl.ds(c0, COLUMNS), :]
                block = lax.dot_general(q, keys, dims, preferred_element_type=jnp.float32)

                def masked(block):
                    column = c0 + lax.broadcasted_iota(jnp.int32, block.shape, 1)
                    return jnp.where(column < length, block, NEG_BIG)

                return lax.cond(c0 + COLUMNS <= length, lambda b: b, masked, block), c0

            draft_scores = lax.dot_general(q, dk_ref[kv], dims, preferred_element_type=jnp.float32)
            draft_keep = dmask_ref[pl.ds(t0, ROW_TOKENS)]
            draft_keep = jnp.broadcast_to(
                draft_keep[:, None, :], (ROW_TOKENS, group, DRAFT_PAD)
            ).reshape(rows, DRAFT_PAD)
            draft_scores = jnp.where(draft_keep > 0.5, draft_scores, NEG_BIG)

            def find_top(c, top):
                block, _ = scores_at(c)
                return jnp.maximum(top, jnp.max(block, axis=-1, keepdims=True))

            top = lax.fori_loop(
                0, steps, find_top, jnp.max(draft_scores, axis=-1, keepdims=True), unroll=True
            )
            safe_top = jnp.maximum(top, NEG_BIG * 0.1)

            def accumulate(c, acc):
                total, numerator = acc
                block, c0 = scores_at(c)
                weight = jnp.exp((block - safe_top) * scale_factor)
                values = v_ref[kv, pl.ds(c0, COLUMNS), :]
                return (
                    total + jnp.sum(weight, axis=-1, keepdims=True),
                    numerator + jnp.dot(
                        weight.astype(jnp.bfloat16), values, preferred_element_type=jnp.float32
                    ),
                )

            draft_weight = jnp.exp((draft_scores - safe_top) * scale_factor)
            start = (
                jnp.sum(draft_weight, axis=-1, keepdims=True),
                jnp.dot(
                    draft_weight.astype(jnp.bfloat16), dv_ref[kv],
                    preferred_element_type=jnp.float32,
                ),
            )
            total, numerator = lax.fori_loop(0, steps, accumulate, start, unroll=True)
            num_ref[pl.ds(t0, ROW_TOKENS), heads, :] = numerator.reshape(
                ROW_TOKENS, group, head_size
            )
            r0 = pl.multiple_of(i * rows, rows)
            top_ref[kv, pl.ds(r0, rows), :] = jnp.broadcast_to(safe_top * scale_factor, (rows, 128))
            tot_ref[kv, pl.ds(r0, rows), :] = jnp.broadcast_to(total, (rows, 128))
            return carry

        lax.fori_loop(0, q_ref.shape[0] // ROW_TOKENS, chunk, 0)


def attend(local_len, queries, cache_keys, cache_values, draft_k, draft_v, draft_mask):
    requests, tree_len, local_heads, head_size = queries.shape
    local_kv = cache_keys.shape[1]
    shard_len = cache_keys.shape[2]
    group = local_heads // local_kv
    kernel = functools.partial(attend_kernel, group=group, local_kv=local_kv)
    stats = jax.ShapeDtypeStruct((requests, local_kv, tree_len * group, 128), jnp.float32)
    grid_spec = pltpu.PrefetchScalarGridSpec(
        num_scalar_prefetch=1,
        grid=(requests,),
        in_specs=[
            pl.BlockSpec((None, tree_len, local_heads, head_size), lambda r, lens: (r, 0, 0, 0)),
            pl.BlockSpec((None, local_kv, shard_len, head_size), lambda r, lens: (r, 0, 0, 0)),
            pl.BlockSpec((None, local_kv, shard_len, head_size), lambda r, lens: (r, 0, 0, 0)),
            pl.BlockSpec((None, local_kv, DRAFT_PAD, head_size), lambda r, lens: (r, 0, 0, 0)),
            pl.BlockSpec((None, local_kv, DRAFT_PAD, head_size), lambda r, lens: (r, 0, 0, 0)),
            pl.BlockSpec((None, tree_len, DRAFT_PAD), lambda r, lens: (r, 0, 0)),
        ],
        out_specs=[
            pl.BlockSpec((None, tree_len, local_heads + 1, head_size),
                         lambda r, lens: (r, 0, 0, 0)),
            pl.BlockSpec((None, local_kv, tree_len * group, 128), lambda r, lens: (r, 0, 0, 0)),
            pl.BlockSpec((None, local_kv, tree_len * group, 128), lambda r, lens: (r, 0, 0, 0)),
        ],
    )
    flops = 4 * requests * tree_len * local_heads * (shard_len + DRAFT_PAD) * head_size
    return pl.pallas_call(
        kernel,
        grid_spec=grid_spec,
        out_shape=[
            jax.ShapeDtypeStruct(
                (requests, tree_len, local_heads + 1, head_size), jnp.float32
            ),
            stats,
            stats,
        ],
        compiler_params=pltpu.CompilerParams(
            dimension_semantics=("arbitrary",),
            vmem_limit_bytes=48 * 1024 * 1024,
        ),
        cost_estimate=pl.CostEstimate(
            flops=flops,
            transcendentals=requests * tree_len * local_heads * (shard_len + DRAFT_PAD),
            bytes_accessed=2 * cache_keys.size * 2 + queries.size * 2 + queries.size * 4,
        ),
    )(local_len, queries, cache_keys, cache_values, draft_k, draft_v, draft_mask)


def local(
    queries, cache_keys, cache_values, lengths, parents, draft_keys, draft_values, out_weight
):
    requests, tree_len, local_heads, head_size = queries.shape
    shard_len = cache_keys.shape[1]
    local_kv = cache_keys.shape[2]
    group = local_heads // local_kv
    draft_len = draft_keys.shape[1]
    seq_size = lax.axis_size("seq")
    seq_index = lax.axis_index("seq")
    tree_mask = ancestry(parents)
    local_len = jnp.clip(lengths - seq_index * shard_len, 0, shard_len).astype(jnp.int32)
    draft_mask = lax.dynamic_slice_in_dim(tree_mask, seq_index * draft_len, draft_len, 2)
    draft_mask = jnp.pad(
        draft_mask.astype(jnp.float32), ((0, 0), (0, 0), (0, DRAFT_PAD - draft_len))
    )
    pad = ((0, 0), (0, 0), (0, DRAFT_PAD - draft_len), (0, 0))
    draft_k = jnp.pad(jnp.transpose(draft_keys, (0, 2, 1, 3)), pad)
    draft_v = jnp.pad(jnp.transpose(draft_values, (0, 2, 1, 3)), pad)
    numerator, top, total = attend(
        local_len, queries, jnp.transpose(cache_keys, (0, 2, 1, 3)),
        jnp.transpose(cache_values, (0, 2, 1, 3)), draft_k, draft_v, draft_mask
    )

    def per_head(stat):
        stat = stat[..., 0].reshape(requests, local_kv, tree_len, group)
        return jnp.transpose(stat, (0, 2, 1, 3)).reshape(requests, tree_len, local_heads)

    seq_size = lax.axis_size("seq")
    rows = requests * tree_len
    top = per_head(top)
    total = per_head(total)
    stats = jnp.concatenate(
        [top, total, jnp.zeros((requests, tree_len, head_size - 2 * local_heads), jnp.float32)],
        axis=-1,
    )
    packed = lax.dynamic_update_slice(numerator, stats[:, :, None, :], (0, 0, local_heads, 0))
    packed = packed.reshape(seq_size, rows // seq_size, local_heads + 1, head_size)
    packed = packed.reshape(seq_size, rows // seq_size, local_heads + 1, head_size)

    def combine(stack):
        common = stack[:, :, local_heads, :local_heads]
        peak = jnp.max(common, axis=0)
        scaling = jnp.exp(common - peak)
        summed_total = jnp.sum(stack[:, :, local_heads, local_heads:2 * local_heads] * scaling,
                               axis=0)
        summed = jnp.sum(stack[:, :, :local_heads, :] * scaling[..., None], axis=0)
        stats = jnp.concatenate(
            [peak, summed_total,
             jnp.zeros(peak.shape[:-1] + (head_size - 2 * local_heads,), jnp.float32)],
            axis=-1,
        )
        return jnp.concatenate([summed, stats[:, None, :]], axis=1)

    inner = 4 if seq_size % 4 == 0 else seq_size
    outer = seq_size // inner
    hi, lo = seq_index // inner, seq_index % inner
    grouped = packed.reshape(outer, inner, rows // seq_size, local_heads + 1, head_size)
    stage = [lax.dynamic_index_in_dim(grouped, lo, 1, keepdims=False)]
    for shift in range(1, inner):
        pairs = [(h * inner + l, h * inner + (l + shift) % inner)
                 for h in range(outer) for l in range(inner)]
        target = (lo + shift) % inner
        stage.append(lax.ppermute(
            lax.dynamic_index_in_dim(grouped, target, 1, keepdims=False), "seq", pairs))
    partial = jnp.stack(
        [combine(jnp.stack([piece[h] for piece in stage], axis=0)) for h in range(outer)], axis=0
    )
    final = [lax.dynamic_index_in_dim(partial, hi, 0, keepdims=False)]
    for shift in range(1, outer):
        pairs = [(h * inner + l, ((h + shift) % outer) * inner + l)
                 for h in range(outer) for l in range(inner)]
        target = (hi + shift) % outer
        final.append(lax.ppermute(
            lax.dynamic_index_in_dim(partial, target, 0, keepdims=False), "seq", pairs))
    mine = combine(jnp.stack(final, axis=0))
    summed = mine[:, :local_heads, :]
    summed_total = mine[:, local_heads, local_heads:2 * local_heads]
    mine_attended = (summed / summed_total[..., None]).astype(jnp.bfloat16)
    across = [mine_attended]
    for shift in range(1, outer):
        pairs = [(h * inner + l, ((h + shift) % outer) * inner + l)
                 for h in range(outer) for l in range(inner)]
        across.append(lax.ppermute(mine_attended, "seq", pairs))
    by_outer = jnp.zeros((outer,) + mine_attended.shape, jnp.bfloat16)
    for shift, piece in enumerate(across):
        by_outer = lax.dynamic_update_index_in_dim(by_outer, piece, (hi - shift) % outer, 0)
    gathered = jnp.zeros((outer, inner) + mine_attended.shape, jnp.bfloat16)
    gathered = lax.dynamic_update_index_in_dim(gathered, by_outer, lo, 1)
    for shift in range(1, inner):
        pairs = [(h * inner + l, h * inner + (l + shift) % inner)
                 for h in range(outer) for l in range(inner)]
        got_piece = lax.ppermute(by_outer, "seq", pairs)
        gathered = lax.dynamic_update_index_in_dim(gathered, got_piece, (lo - shift) % inner, 1)
    attended = gathered
    attended = attended.reshape(requests * tree_len, local_heads * head_size)
    terms = jnp.dot(attended, out_weight, preferred_element_type=jnp.float32)
    head_count = lax.axis_size("head")
    if head_count & (head_count - 1):
        return lax.psum_scatter(terms, "head", scatter_dimension=1, tiled=True).astype(
            jnp.bfloat16
        )
    head_index = lax.axis_index("head")
    width = terms.shape[1] // head_count
    kept = lax.optimization_barrier(terms).reshape(rows, head_count, width)
    bit = 1
    while bit < head_count:
        mine_bit = (head_index // bit) % 2
        halves = kept.reshape(rows, kept.shape[1] // 2, 2, width)
        keep = lax.dynamic_index_in_dim(halves, mine_bit, 2, keepdims=False)
        send = lax.dynamic_index_in_dim(halves, 1 - mine_bit, 2, keepdims=False)
        kept = keep + lax.ppermute(send, "head", [(i, i ^ bit) for i in range(head_count)])
        bit *= 2
    return kept.reshape(rows, width).astype(jnp.bfloat16)


def solution(mesh):
    return jax.shard_map(
        local,
        mesh=mesh,
        in_specs=(
            P(None, None, "head", None),
            P(None, "seq", "head", None),
            P(None, "seq", "head", None),
            P(),
            P(),
            P(None, "seq", "head", None),
            P(None, "seq", "head", None),
            P("head", "seq"),
        ),
        out_specs=P(None, ("seq", "head")),
        check_vma=False,
    )
```

```python
import functools

import jax
import jax.numpy as jnp
from jax import lax
from jax.experimental import pallas as pl
from jax.experimental.pallas import tpu as pltpu
from jax.sharding import PartitionSpec as P

NEG_BIG = -1e30
DRAFT_PAD = 128
ROW_TOKENS = 8
COLUMNS = 256


def ancestry(parents):
    tree_len = parents.shape[1]
    columns = jnp.arange(tree_len, dtype=jnp.int32)
    linked = (parents[:, :, None] == columns[None, None, :]) | (
        columns[:, None] == columns[None, :]
    )[None, :, :]
    reach = linked.astype(jnp.float32)
    for step in range(tree_len.bit_length()):
        reach = jnp.minimum(
            jnp.einsum("rij,rjk->rik", reach, reach, precision=lax.Precision.HIGHEST), 1.0
        )
    return reach > 0.5


def attend_kernel(lens_ref, q_ref, k_ref, v_ref, dk_ref, dv_ref, dmask_ref,
                  num_ref, top_ref, tot_ref, *, group, local_kv):
    r = pl.program_id(0)
    length = lens_ref[r]
    head_size = q_ref.shape[-1]
    shard_len = k_ref.shape[1]
    scale_factor = head_size ** (-0.5)
    rows = ROW_TOKENS * group
    dims = (((1,), (1,)), ((), ()))
    steps = shard_len // COLUMNS

    for kv in range(local_kv):
        heads = pl.ds(kv * group, group)

        def chunk(i, carry, kv=kv, heads=heads):
            t0 = pl.multiple_of(i * ROW_TOKENS, ROW_TOKENS)
            q = q_ref[pl.ds(t0, ROW_TOKENS), heads, :].reshape(rows, head_size)

            def scores_at(c):
                c0 = pl.multiple_of(c * COLUMNS, COLUMNS)
                keys = k_ref[kv, pl.ds(c0, COLUMNS), :]
                block = lax.dot_general(q, keys, dims, preferred_element_type=jnp.float32)

                def masked(block):
                    column = c0 + lax.broadcasted_iota(jnp.int32, block.shape, 1)
                    return jnp.where(column < length, block, NEG_BIG)

                return lax.cond(c0 + COLUMNS <= length, lambda b: b, masked, block), c0

            draft_scores = lax.dot_general(q, dk_ref[kv], dims, preferred_element_type=jnp.float32)
            draft_keep = dmask_ref[pl.ds(t0, ROW_TOKENS)]
            draft_keep = jnp.broadcast_to(
                draft_keep[:, None, :], (ROW_TOKENS, group, DRAFT_PAD)
            ).reshape(rows, DRAFT_PAD)
            draft_scores = jnp.where(draft_keep > 0.5, draft_scores, NEG_BIG)

            def find_top(c, top):
                block, _ = scores_at(c)
                return jnp.maximum(top, jnp.max(block, axis=-1, keepdims=True))

            top = lax.fori_loop(
                0, steps, find_top, jnp.max(draft_scores, axis=-1, keepdims=True), unroll=True
            )
            safe_top = jnp.maximum(top, NEG_BIG * 0.1)

            def accumulate(c, acc):
                total, numerator = acc
                block, c0 = scores_at(c)
                weight = jnp.exp((block - safe_top) * scale_factor)
                values = v_ref[kv, pl.ds(c0, COLUMNS), :]
                return (
                    total + jnp.sum(weight, axis=-1, keepdims=True),
                    numerator + jnp.dot(
                        weight.astype(jnp.bfloat16), values, preferred_element_type=jnp.float32
                    ),
                )

            draft_weight = jnp.exp((draft_scores - safe_top) * scale_factor)
            start = (
                jnp.sum(draft_weight, axis=-1, keepdims=True),
                jnp.dot(
                    draft_weight.astype(jnp.bfloat16), dv_ref[kv],
                    preferred_element_type=jnp.float32,
                ),
            )
            total, numerator = lax.fori_loop(0, steps, accumulate, start, unroll=True)
            num_ref[pl.ds(t0, ROW_TOKENS), heads, :] = numerator.reshape(
                ROW_TOKENS, group, head_size
            )
            r0 = pl.multiple_of(i * rows, rows)
            top_ref[kv, pl.ds(r0, rows), :] = jnp.broadcast_to(safe_top * scale_factor, (rows, 128))
            tot_ref[kv, pl.ds(r0, rows), :] = jnp.broadcast_to(total, (rows, 128))
            return carry

        lax.fori_loop(0, q_ref.shape[0] // ROW_TOKENS, chunk, 0, unroll=2)


def attend(local_len, queries, cache_keys, cache_values, draft_k, draft_v, draft_mask):
    requests, tree_len, local_heads, head_size = queries.shape
    local_kv = cache_keys.shape[1]
    shard_len = cache_keys.shape[2]
    group = local_heads // local_kv
    kernel = functools.partial(attend_kernel, group=group, local_kv=local_kv)
    stats = jax.ShapeDtypeStruct((requests, local_kv, tree_len * group, 128), jnp.float32)
    grid_spec = pltpu.PrefetchScalarGridSpec(
        num_scalar_prefetch=1,
        grid=(requests,),
        in_specs=[
            pl.BlockSpec((None, tree_len, local_heads, head_size), lambda r, lens: (r, 0, 0, 0)),
            pl.BlockSpec((None, local_kv, shard_len, head_size), lambda r, lens: (r, 0, 0, 0)),
            pl.BlockSpec((None, local_kv, shard_len, head_size), lambda r, lens: (r, 0, 0, 0)),
            pl.BlockSpec((None, local_kv, DRAFT_PAD, head_size), lambda r, lens: (r, 0, 0, 0)),
            pl.BlockSpec((None, local_kv, DRAFT_PAD, head_size), lambda r, lens: (r, 0, 0, 0)),
            pl.BlockSpec((None, tree_len, DRAFT_PAD), lambda r, lens: (r, 0, 0)),
        ],
        out_specs=[
            pl.BlockSpec((None, tree_len, local_heads + 1, head_size),
                         lambda r, lens: (r, 0, 0, 0)),
            pl.BlockSpec((None, local_kv, tree_len * group, 128), lambda r, lens: (r, 0, 0, 0)),
            pl.BlockSpec((None, local_kv, tree_len * group, 128), lambda r, lens: (r, 0, 0, 0)),
        ],
    )
    flops = 4 * requests * tree_len * local_heads * (shard_len + DRAFT_PAD) * head_size
    return pl.pallas_call(
        kernel,
        grid_spec=grid_spec,
        out_shape=[
            jax.ShapeDtypeStruct(
                (requests, tree_len, local_heads + 1, head_size), jnp.float32
            ),
            stats,
            stats,
        ],
        compiler_params=pltpu.CompilerParams(
            dimension_semantics=("arbitrary",),
            vmem_limit_bytes=48 * 1024 * 1024,
        ),
        cost_estimate=pl.CostEstimate(
            flops=flops,
            transcendentals=requests * tree_len * local_heads * (shard_len + DRAFT_PAD),
            bytes_accessed=2 * cache_keys.size * 2 + queries.size * 2 + queries.size * 4,
        ),
    )(local_len, queries, cache_keys, cache_values, draft_k, draft_v, draft_mask)


def local(
    queries, cache_keys, cache_values, lengths, parents, draft_keys, draft_values, out_weight
):
    requests, tree_len, local_heads, head_size = queries.shape
    shard_len = cache_keys.shape[1]
    local_kv = cache_keys.shape[2]
    group = local_heads // local_kv
    draft_len = draft_keys.shape[1]
    seq_size = lax.axis_size("seq")
    seq_index = lax.axis_index("seq")
    tree_mask = ancestry(parents)
    local_len = jnp.clip(lengths - seq_index * shard_len, 0, shard_len).astype(jnp.int32)
    draft_mask = lax.dynamic_slice_in_dim(tree_mask, seq_index * draft_len, draft_len, 2)
    draft_mask = jnp.pad(
        draft_mask.astype(jnp.float32), ((0, 0), (0, 0), (0, DRAFT_PAD - draft_len))
    )
    pad = ((0, 0), (0, 0), (0, DRAFT_PAD - draft_len), (0, 0))
    draft_k = jnp.pad(jnp.transpose(draft_keys, (0, 2, 1, 3)), pad)
    draft_v = jnp.pad(jnp.transpose(draft_values, (0, 2, 1, 3)), pad)
    numerator, top, total = attend(
        local_len, queries, jnp.transpose(cache_keys, (0, 2, 1, 3)),
        jnp.transpose(cache_values, (0, 2, 1, 3)), draft_k, draft_v, draft_mask
    )

    def per_head(stat):
        stat = stat[..., 0].reshape(requests, local_kv, tree_len, group)
        return jnp.transpose(stat, (0, 2, 1, 3)).reshape(requests, tree_len, local_heads)

    seq_size = lax.axis_size("seq")
    rows = requests * tree_len
    top = per_head(top)
    total = per_head(total)
    stats = jnp.concatenate(
        [top, total, jnp.zeros((requests, tree_len, head_size - 2 * local_heads), jnp.float32)],
        axis=-1,
    )
    packed = lax.dynamic_update_slice(numerator, stats[:, :, None, :], (0, 0, local_heads, 0))
    packed = packed.reshape(seq_size, rows // seq_size, local_heads + 1, head_size)
    packed = packed.reshape(seq_size, rows // seq_size, local_heads + 1, head_size)

    def combine(stack):
        common = stack[:, :, local_heads, :local_heads]
        peak = jnp.max(common, axis=0)
        scaling = jnp.exp(common - peak)
        summed_total = jnp.sum(stack[:, :, local_heads, local_heads:2 * local_heads] * scaling,
                               axis=0)
        summed = jnp.sum(stack[:, :, :local_heads, :] * scaling[..., None], axis=0)
        stats = jnp.concatenate(
            [peak, summed_total,
             jnp.zeros(peak.shape[:-1] + (head_size - 2 * local_heads,), jnp.float32)],
            axis=-1,
        )
        return jnp.concatenate([summed, stats[:, None, :]], axis=1)

    inner = 4 if seq_size % 4 == 0 else seq_size
    outer = seq_size // inner
    hi, lo = seq_index // inner, seq_index % inner
    grouped = packed.reshape(outer, inner, rows // seq_size, local_heads + 1, head_size)
    stage = [lax.dynamic_index_in_dim(grouped, lo, 1, keepdims=False)]
    for shift in range(1, inner):
        pairs = [(h * inner + l, h * inner + (l + shift) % inner)
                 for h in range(outer) for l in range(inner)]
        target = (lo + shift) % inner
        stage.append(lax.ppermute(
            lax.dynamic_index_in_dim(grouped, target, 1, keepdims=False), "seq", pairs))
    partial = jnp.stack(
        [combine(jnp.stack([piece[h] for piece in stage], axis=0)) for h in range(outer)], axis=0
    )
    final = [lax.dynamic_index_in_dim(partial, hi, 0, keepdims=False)]
    for shift in range(1, outer):
        pairs = [(h * inner + l, ((h + shift) % outer) * inner + l)
                 for h in range(outer) for l in range(inner)]
        target = (hi + shift) % outer
        final.append(lax.ppermute(
            lax.dynamic_index_in_dim(partial, target, 0, keepdims=False), "seq", pairs))
    mine = combine(jnp.stack(final, axis=0))
    summed = mine[:, :local_heads, :]
    summed_total = mine[:, local_heads, local_heads:2 * local_heads]
    mine_attended = (summed / summed_total[..., None]).astype(jnp.bfloat16)
    across = [mine_attended]
    for shift in range(1, outer):
        pairs = [(h * inner + l, ((h + shift) % outer) * inner + l)
                 for h in range(outer) for l in range(inner)]
        across.append(lax.ppermute(mine_attended, "seq", pairs))
    by_outer = jnp.zeros((outer,) + mine_attended.shape, jnp.bfloat16)
    for shift, piece in enumerate(across):
        by_outer = lax.dynamic_update_index_in_dim(by_outer, piece, (hi - shift) % outer, 0)
    gathered = jnp.zeros((outer, inner) + mine_attended.shape, jnp.bfloat16)
    gathered = lax.dynamic_update_index_in_dim(gathered, by_outer, lo, 1)
    for shift in range(1, inner):
        pairs = [(h * inner + l, h * inner + (l + shift) % inner)
                 for h in range(outer) for l in range(inner)]
        got_piece = lax.ppermute(by_outer, "seq", pairs)
        gathered = lax.dynamic_update_index_in_dim(gathered, got_piece, (lo - shift) % inner, 1)
    attended = gathered
    attended = attended.reshape(requests * tree_len, local_heads * head_size)
    terms = jnp.dot(attended, out_weight, preferred_element_type=jnp.float32)
    head_count = lax.axis_size("head")
    if head_count & (head_count - 1):
        return lax.psum_scatter(terms, "head", scatter_dimension=1, tiled=True).astype(
            jnp.bfloat16
        )
    head_index = lax.axis_index("head")
    width = terms.shape[1] // head_count
    kept = lax.optimization_barrier(terms).reshape(rows, head_count, width)
    bit = 1
    while bit < head_count:
        mine_bit = (head_index // bit) % 2
        halves = kept.reshape(rows, kept.shape[1] // 2, 2, width)
        keep = lax.dynamic_index_in_dim(halves, mine_bit, 2, keepdims=False)
        send = lax.dynamic_index_in_dim(halves, 1 - mine_bit, 2, keepdims=False)
        kept = keep + lax.ppermute(send, "head", [(i, i ^ bit) for i in range(head_count)])
        bit *= 2
    return kept.reshape(rows, width).astype(jnp.bfloat16)


def solution(mesh):
    return jax.shard_map(
        local,
        mesh=mesh,
        in_specs=(
            P(None, None, "head", None),
            P(None, "seq", "head", None),
            P(None, "seq", "head", None),
            P(),
            P(),
            P(None, "seq", "head", None),
            P(None, "seq", "head", None),
            P("head", "seq"),
        ),
        out_specs=P(None, ("seq", "head")),
        check_vma=False,
    )
```

```python
import functools

import jax
import jax.numpy as jnp
from jax import lax
from jax.experimental import pallas as pl
from jax.experimental.pallas import tpu as pltpu
from jax.sharding import PartitionSpec as P

NEG_BIG = -1e30
DRAFT_PAD = 128
ROW_TOKENS = 8
COLUMNS = 256


def ancestry(parents):
    tree_len = parents.shape[1]
    columns = jnp.arange(tree_len, dtype=jnp.int32)
    linked = (parents[:, :, None] == columns[None, None, :]) | (
        columns[:, None] == columns[None, :]
    )[None, :, :]
    reach = linked.astype(jnp.float32)
    for step in range(tree_len.bit_length()):
        reach = jnp.minimum(
            jnp.einsum("rij,rjk->rik", reach, reach, precision=lax.Precision.HIGHEST), 1.0
        )
    return reach > 0.5


def attend_kernel(lens_ref, q_ref, k_ref, v_ref, dk_ref, dv_ref, dmask_ref,
                  num_ref, top_ref, tot_ref, *, group, local_kv):
    r = pl.program_id(0)
    length = lens_ref[r]
    head_size = q_ref.shape[-1]
    shard_len = k_ref.shape[1]
    scale_factor = head_size ** (-0.5)
    rows = ROW_TOKENS * group
    dims = (((1,), (1,)), ((), ()))
    steps = shard_len // COLUMNS

    for kv in range(local_kv):
        heads = pl.ds(kv * group, group)

        def chunk(i, carry, kv=kv, heads=heads):
            t0 = pl.multiple_of(i * ROW_TOKENS, ROW_TOKENS)
            q = q_ref[pl.ds(t0, ROW_TOKENS), heads, :].reshape(rows, head_size)

            def scores_at(c):
                c0 = pl.multiple_of(c * COLUMNS, COLUMNS)
                keys = k_ref[kv, pl.ds(c0, COLUMNS), :]
                block = lax.dot_general(q, keys, dims, preferred_element_type=jnp.float32)

                def masked(block):
                    column = c0 + lax.broadcasted_iota(jnp.int32, block.shape, 1)
                    return jnp.where(column < length, block, NEG_BIG)

                return lax.cond(c0 + COLUMNS <= length, lambda b: b, masked, block), c0

            draft_scores = lax.dot_general(q, dk_ref[kv], dims, preferred_element_type=jnp.float32)
            draft_keep = dmask_ref[pl.ds(t0, ROW_TOKENS)]
            draft_keep = jnp.broadcast_to(
                draft_keep[:, None, :], (ROW_TOKENS, group, DRAFT_PAD)
            ).reshape(rows, DRAFT_PAD)
            draft_scores = jnp.where(draft_keep > 0.5, draft_scores, NEG_BIG)

            def find_top(c, top):
                block, _ = scores_at(c)
                return jnp.maximum(top, jnp.max(block, axis=-1, keepdims=True))

            top = lax.fori_loop(
                0, steps, find_top, jnp.max(draft_scores, axis=-1, keepdims=True), unroll=True
            )
            safe_top = jnp.maximum(top, NEG_BIG * 0.1)

            def accumulate(c, acc):
                total, numerator = acc
                block, c0 = scores_at(c)
                weight = jnp.exp((block - safe_top) * scale_factor)
                values = v_ref[kv, pl.ds(c0, COLUMNS), :]
                return (
                    total + jnp.sum(weight, axis=-1, keepdims=True),
                    numerator + jnp.dot(
                        weight.astype(jnp.bfloat16), values, preferred_element_type=jnp.float32
                    ),
                )

            draft_weight = jnp.exp((draft_scores - safe_top) * scale_factor)
            start = (
                jnp.sum(draft_weight, axis=-1, keepdims=True),
                jnp.dot(
                    draft_weight.astype(jnp.bfloat16), dv_ref[kv],
                    preferred_element_type=jnp.float32,
                ),
            )
            total, numerator = lax.fori_loop(0, steps, accumulate, start, unroll=True)
            num_ref[pl.ds(t0, ROW_TOKENS), heads, :] = numerator.reshape(
                ROW_TOKENS, group, head_size
            )
            r0 = pl.multiple_of(i * rows, rows)
            top_ref[kv, pl.ds(r0, rows), :] = jnp.broadcast_to(safe_top * scale_factor, (rows, 128))
            tot_ref[kv, pl.ds(r0, rows), :] = jnp.broadcast_to(total, (rows, 128))
            return carry

        lax.fori_loop(0, q_ref.shape[0] // ROW_TOKENS, chunk, 0, unroll=True)


def attend(local_len, queries, cache_keys, cache_values, draft_k, draft_v, draft_mask):
    requests, tree_len, local_heads, head_size = queries.shape
    local_kv = cache_keys.shape[1]
    shard_len = cache_keys.shape[2]
    group = local_heads // local_kv
    kernel = functools.partial(attend_kernel, group=group, local_kv=local_kv)
    stats = jax.ShapeDtypeStruct((requests, local_kv, tree_len * group, 128), jnp.float32)
    grid_spec = pltpu.PrefetchScalarGridSpec(
        num_scalar_prefetch=1,
        grid=(requests,),
        in_specs=[
            pl.BlockSpec((None, tree_len, local_heads, head_size), lambda r, lens: (r, 0, 0, 0)),
            pl.BlockSpec((None, local_kv, shard_len, head_size), lambda r, lens: (r, 0, 0, 0)),
            pl.BlockSpec((None, local_kv, shard_len, head_size), lambda r, lens: (r, 0, 0, 0)),
            pl.BlockSpec((None, local_kv, DRAFT_PAD, head_size), lambda r, lens: (r, 0, 0, 0)),
            pl.BlockSpec((None, local_kv, DRAFT_PAD, head_size), lambda r, lens: (r, 0, 0, 0)),
            pl.BlockSpec((None, tree_len, DRAFT_PAD), lambda r, lens: (r, 0, 0)),
        ],
        out_specs=[
            pl.BlockSpec((None, tree_len, local_heads + 1, head_size),
                         lambda r, lens: (r, 0, 0, 0)),
            pl.BlockSpec((None, local_kv, tree_len * group, 128), lambda r, lens: (r, 0, 0, 0)),
            pl.BlockSpec((None, local_kv, tree_len * group, 128), lambda r, lens: (r, 0, 0, 0)),
        ],
    )
    flops = 4 * requests * tree_len * local_heads * (shard_len + DRAFT_PAD) * head_size
    return pl.pallas_call(
        kernel,
        grid_spec=grid_spec,
        out_shape=[
            jax.ShapeDtypeStruct(
                (requests, tree_len, local_heads + 1, head_size), jnp.float32
            ),
            stats,
            stats,
        ],
        compiler_params=pltpu.CompilerParams(
            dimension_semantics=("arbitrary",),
            vmem_limit_bytes=48 * 1024 * 1024,
        ),
        cost_estimate=pl.CostEstimate(
            flops=flops,
            transcendentals=requests * tree_len * local_heads * (shard_len + DRAFT_PAD),
            bytes_accessed=2 * cache_keys.size * 2 + queries.size * 2 + queries.size * 4,
        ),
    )(local_len, queries, cache_keys, cache_values, draft_k, draft_v, draft_mask)


def local(
    queries, cache_keys, cache_values, lengths, parents, draft_keys, draft_values, out_weight
):
    requests, tree_len, local_heads, head_size = queries.shape
    shard_len = cache_keys.shape[1]
    local_kv = cache_keys.shape[2]
    group = local_heads // local_kv
    draft_len = draft_keys.shape[1]
    seq_size = lax.axis_size("seq")
    seq_index = lax.axis_index("seq")
    tree_mask = ancestry(parents)
    local_len = jnp.clip(lengths - seq_index * shard_len, 0, shard_len).astype(jnp.int32)
    draft_mask = lax.dynamic_slice_in_dim(tree_mask, seq_index * draft_len, draft_len, 2)
    draft_mask = jnp.pad(
        draft_mask.astype(jnp.float32), ((0, 0), (0, 0), (0, DRAFT_PAD - draft_len))
    )
    pad = ((0, 0), (0, 0), (0, DRAFT_PAD - draft_len), (0, 0))
    draft_k = jnp.pad(jnp.transpose(draft_keys, (0, 2, 1, 3)), pad)
    draft_v = jnp.pad(jnp.transpose(draft_values, (0, 2, 1, 3)), pad)
    numerator, top, total = attend(
        local_len, queries, jnp.transpose(cache_keys, (0, 2, 1, 3)),
        jnp.transpose(cache_values, (0, 2, 1, 3)), draft_k, draft_v, draft_mask
    )

    def per_head(stat):
        stat = stat[..., 0].reshape(requests, local_kv, tree_len, group)
        return jnp.transpose(stat, (0, 2, 1, 3)).reshape(requests, tree_len, local_heads)

    seq_size = lax.axis_size("seq")
    rows = requests * tree_len
    top = per_head(top)
    total = per_head(total)
    stats = jnp.concatenate(
        [top, total, jnp.zeros((requests, tree_len, head_size - 2 * local_heads), jnp.float32)],
        axis=-1,
    )
    packed = lax.dynamic_update_slice(numerator, stats[:, :, None, :], (0, 0, local_heads, 0))
    packed = packed.reshape(seq_size, rows // seq_size, local_heads + 1, head_size)
    packed = packed.reshape(seq_size, rows // seq_size, local_heads + 1, head_size)

    def combine(stack):
        common = stack[:, :, local_heads, :local_heads]
        peak = jnp.max(common, axis=0)
        scaling = jnp.exp(common - peak)
        summed_total = jnp.sum(stack[:, :, local_heads, local_heads:2 * local_heads] * scaling,
                               axis=0)
        summed = jnp.sum(stack[:, :, :local_heads, :] * scaling[..., None], axis=0)
        stats = jnp.concatenate(
            [peak, summed_total,
             jnp.zeros(peak.shape[:-1] + (head_size - 2 * local_heads,), jnp.float32)],
            axis=-1,
        )
        return jnp.concatenate([summed, stats[:, None, :]], axis=1)

    inner = 4 if seq_size % 4 == 0 else seq_size
    outer = seq_size // inner
    hi, lo = seq_index // inner, seq_index % inner
    grouped = packed.reshape(outer, inner, rows // seq_size, local_heads + 1, head_size)
    stage = [lax.dynamic_index_in_dim(grouped, lo, 1, keepdims=False)]
    for shift in range(1, inner):
        pairs = [(h * inner + l, h * inner + (l + shift) % inner)
                 for h in range(outer) for l in range(inner)]
        target = (lo + shift) % inner
        stage.append(lax.ppermute(
            lax.dynamic_index_in_dim(grouped, target, 1, keepdims=False), "seq", pairs))
    partial = jnp.stack(
        [combine(jnp.stack([piece[h] for piece in stage], axis=0)) for h in range(outer)], axis=0
    )
    final = [lax.dynamic_index_in_dim(partial, hi, 0, keepdims=False)]
    for shift in range(1, outer):
        pairs = [(h * inner + l, ((h + shift) % outer) * inner + l)
                 for h in range(outer) for l in range(inner)]
        target = (hi + shift) % outer
        final.append(lax.ppermute(
            lax.dynamic_index_in_dim(partial, target, 0, keepdims=False), "seq", pairs))
    mine = combine(jnp.stack(final, axis=0))
    summed = mine[:, :local_heads, :]
    summed_total = mine[:, local_heads, local_heads:2 * local_heads]
    mine_attended = (summed / summed_total[..., None]).astype(jnp.bfloat16)
    across = [mine_attended]
    for shift in range(1, outer):
        pairs = [(h * inner + l, ((h + shift) % outer) * inner + l)
                 for h in range(outer) for l in range(inner)]
        across.append(lax.ppermute(mine_attended, "seq", pairs))
    by_outer = jnp.zeros((outer,) + mine_attended.shape, jnp.bfloat16)
    for shift, piece in enumerate(across):
        by_outer = lax.dynamic_update_index_in_dim(by_outer, piece, (hi - shift) % outer, 0)
    gathered = jnp.zeros((outer, inner) + mine_attended.shape, jnp.bfloat16)
    gathered = lax.dynamic_update_index_in_dim(gathered, by_outer, lo, 1)
    for shift in range(1, inner):
        pairs = [(h * inner + l, h * inner + (l + shift) % inner)
                 for h in range(outer) for l in range(inner)]
        got_piece = lax.ppermute(by_outer, "seq", pairs)
        gathered = lax.dynamic_update_index_in_dim(gathered, got_piece, (lo - shift) % inner, 1)
    attended = gathered
    attended = attended.reshape(requests * tree_len, local_heads * head_size)
    terms = jnp.dot(attended, out_weight, preferred_element_type=jnp.float32)
    head_count = lax.axis_size("head")
    if head_count & (head_count - 1):
        return lax.psum_scatter(terms, "head", scatter_dimension=1, tiled=True).astype(
            jnp.bfloat16
        )
    head_index = lax.axis_index("head")
    width = terms.shape[1] // head_count
    kept = lax.optimization_barrier(terms).reshape(rows, head_count, width)
    bit = 1
    while bit < head_count:
        mine_bit = (head_index // bit) % 2
        halves = kept.reshape(rows, kept.shape[1] // 2, 2, width)
        keep = lax.dynamic_index_in_dim(halves, mine_bit, 2, keepdims=False)
        send = lax.dynamic_index_in_dim(halves, 1 - mine_bit, 2, keepdims=False)
        kept = keep + lax.ppermute(send, "head", [(i, i ^ bit) for i in range(head_count)])
        bit *= 2
    return kept.reshape(rows, width).astype(jnp.bfloat16)


def solution(mesh):
    return jax.shard_map(
        local,
        mesh=mesh,
        in_specs=(
            P(None, None, "head", None),
            P(None, "seq", "head", None),
            P(None, "seq", "head", None),
            P(),
            P(),
            P(None, "seq", "head", None),
            P(None, "seq", "head", None),
            P("head", "seq"),
        ),
        out_specs=P(None, ("seq", "head")),
        check_vma=False,
    )
```

```python
import functools

import jax
import jax.numpy as jnp
from jax import lax
from jax.experimental import pallas as pl
from jax.experimental.pallas import tpu as pltpu
from jax.sharding import PartitionSpec as P

NEG_BIG = -1e30
DRAFT_PAD = 128
ROW_TOKENS = 8
COLUMNS = 256


def ancestry(parents):
    tree_len = parents.shape[1]
    columns = jnp.arange(tree_len, dtype=jnp.int32)
    linked = (parents[:, :, None] == columns[None, None, :]) | (
        columns[:, None] == columns[None, :]
    )[None, :, :]
    reach = linked.astype(jnp.float32)
    for step in range(tree_len.bit_length()):
        reach = jnp.minimum(
            jnp.einsum("rij,rjk->rik", reach, reach, precision=lax.Precision.HIGHEST), 1.0
        )
    return reach > 0.5


def attend_kernel(lens_ref, q_ref, k_ref, v_ref, dk_ref, dv_ref, dmask_ref,
                  num_ref, top_ref, tot_ref, *, group, local_kv):
    r = pl.program_id(0)
    length = lens_ref[r]
    head_size = q_ref.shape[-1]
    shard_len = k_ref.shape[1]
    scale_factor = head_size ** (-0.5)
    rows = ROW_TOKENS * group
    dims = (((1,), (1,)), ((), ()))
    steps = shard_len // COLUMNS

    for kv in range(local_kv):
        heads = pl.ds(kv * group, group)

        def chunk(i, carry, kv=kv, heads=heads):
            t0 = pl.multiple_of(i * ROW_TOKENS, ROW_TOKENS)
            q = q_ref[pl.ds(t0, ROW_TOKENS), heads, :].reshape(rows, head_size)

            def scores_at(c):
                c0 = pl.multiple_of(c * COLUMNS, COLUMNS)
                keys = k_ref[kv, pl.ds(c0, COLUMNS), :]
                block = lax.dot_general(q, keys, dims, preferred_element_type=jnp.float32)

                column = c0 + lax.broadcasted_iota(jnp.int32, block.shape, 1)
                return jnp.where(column < length, block, NEG_BIG), c0

            draft_scores = lax.dot_general(q, dk_ref[kv], dims, preferred_element_type=jnp.float32)
            draft_keep = dmask_ref[pl.ds(t0, ROW_TOKENS)]
            draft_keep = jnp.broadcast_to(
                draft_keep[:, None, :], (ROW_TOKENS, group, DRAFT_PAD)
            ).reshape(rows, DRAFT_PAD)
            draft_scores = jnp.where(draft_keep > 0.5, draft_scores, NEG_BIG)

            def find_top(c, top):
                block, _ = scores_at(c)
                return jnp.maximum(top, jnp.max(block, axis=-1, keepdims=True))

            top = lax.fori_loop(
                0, steps, find_top, jnp.max(draft_scores, axis=-1, keepdims=True), unroll=True
            )
            safe_top = jnp.maximum(top, NEG_BIG * 0.1)

            def accumulate(c, acc):
                total, numerator = acc
                block, c0 = scores_at(c)
                weight = jnp.exp((block - safe_top) * scale_factor)
                values = v_ref[kv, pl.ds(c0, COLUMNS), :]
                return (
                    total + jnp.sum(weight, axis=-1, keepdims=True),
                    numerator + jnp.dot(
                        weight.astype(jnp.bfloat16), values, preferred_element_type=jnp.float32
                    ),
                )

            draft_weight = jnp.exp((draft_scores - safe_top) * scale_factor)
            start = (
                jnp.sum(draft_weight, axis=-1, keepdims=True),
                jnp.dot(
                    draft_weight.astype(jnp.bfloat16), dv_ref[kv],
                    preferred_element_type=jnp.float32,
                ),
            )
            total, numerator = lax.fori_loop(0, steps, accumulate, start, unroll=True)
            num_ref[pl.ds(t0, ROW_TOKENS), heads, :] = numerator.reshape(
                ROW_TOKENS, group, head_size
            )
            r0 = pl.multiple_of(i * rows, rows)
            top_ref[kv, pl.ds(r0, rows), :] = jnp.broadcast_to(safe_top * scale_factor, (rows, 128))
            tot_ref[kv, pl.ds(r0, rows), :] = jnp.broadcast_to(total, (rows, 128))
            return carry

        lax.fori_loop(0, q_ref.shape[0] // ROW_TOKENS, chunk, 0, unroll=True)


def attend(local_len, queries, cache_keys, cache_values, draft_k, draft_v, draft_mask):
    requests, tree_len, local_heads, head_size = queries.shape
    local_kv = cache_keys.shape[1]
    shard_len = cache_keys.shape[2]
    group = local_heads // local_kv
    kernel = functools.partial(attend_kernel, group=group, local_kv=local_kv)
    stats = jax.ShapeDtypeStruct((requests, local_kv, tree_len * group, 128), jnp.float32)
    grid_spec = pltpu.PrefetchScalarGridSpec(
        num_scalar_prefetch=1,
        grid=(requests,),
        in_specs=[
            pl.BlockSpec((None, tree_len, local_heads, head_size), lambda r, lens: (r, 0, 0, 0)),
            pl.BlockSpec((None, local_kv, shard_len, head_size), lambda r, lens: (r, 0, 0, 0)),
            pl.BlockSpec((None, local_kv, shard_len, head_size), lambda r, lens: (r, 0, 0, 0)),
            pl.BlockSpec((None, local_kv, DRAFT_PAD, head_size), lambda r, lens: (r, 0, 0, 0)),
            pl.BlockSpec((None, local_kv, DRAFT_PAD, head_size), lambda r, lens: (r, 0, 0, 0)),
            pl.BlockSpec((None, tree_len, DRAFT_PAD), lambda r, lens: (r, 0, 0)),
        ],
        out_specs=[
            pl.BlockSpec((None, tree_len, local_heads + 1, head_size),
                         lambda r, lens: (r, 0, 0, 0)),
            pl.BlockSpec((None, local_kv, tree_len * group, 128), lambda r, lens: (r, 0, 0, 0)),
            pl.BlockSpec((None, local_kv, tree_len * group, 128), lambda r, lens: (r, 0, 0, 0)),
        ],
    )
    flops = 4 * requests * tree_len * local_heads * (shard_len + DRAFT_PAD) * head_size
    return pl.pallas_call(
        kernel,
        grid_spec=grid_spec,
        out_shape=[
            jax.ShapeDtypeStruct(
                (requests, tree_len, local_heads + 1, head_size), jnp.float32
            ),
            stats,
            stats,
        ],
        compiler_params=pltpu.CompilerParams(
            dimension_semantics=("arbitrary",),
            vmem_limit_bytes=48 * 1024 * 1024,
        ),
        cost_estimate=pl.CostEstimate(
            flops=flops,
            transcendentals=requests * tree_len * local_heads * (shard_len + DRAFT_PAD),
            bytes_accessed=2 * cache_keys.size * 2 + queries.size * 2 + queries.size * 4,
        ),
    )(local_len, queries, cache_keys, cache_values, draft_k, draft_v, draft_mask)


def local(
    queries, cache_keys, cache_values, lengths, parents, draft_keys, draft_values, out_weight
):
    requests, tree_len, local_heads, head_size = queries.shape
    shard_len = cache_keys.shape[1]
    local_kv = cache_keys.shape[2]
    group = local_heads // local_kv
    draft_len = draft_keys.shape[1]
    seq_size = lax.axis_size("seq")
    seq_index = lax.axis_index("seq")
    tree_mask = ancestry(parents)
    local_len = jnp.clip(lengths - seq_index * shard_len, 0, shard_len).astype(jnp.int32)
    draft_mask = lax.dynamic_slice_in_dim(tree_mask, seq_index * draft_len, draft_len, 2)
    draft_mask = jnp.pad(
        draft_mask.astype(jnp.float32), ((0, 0), (0, 0), (0, DRAFT_PAD - draft_len))
    )
    pad = ((0, 0), (0, 0), (0, DRAFT_PAD - draft_len), (0, 0))
    draft_k = jnp.pad(jnp.transpose(draft_keys, (0, 2, 1, 3)), pad)
    draft_v = jnp.pad(jnp.transpose(draft_values, (0, 2, 1, 3)), pad)
    numerator, top, total = attend(
        local_len, queries, jnp.transpose(cache_keys, (0, 2, 1, 3)),
        jnp.transpose(cache_values, (0, 2, 1, 3)), draft_k, draft_v, draft_mask
    )

    def per_head(stat):
        stat = stat[..., 0].reshape(requests, local_kv, tree_len, group)
        return jnp.transpose(stat, (0, 2, 1, 3)).reshape(requests, tree_len, local_heads)

    seq_size = lax.axis_size("seq")
    rows = requests * tree_len
    top = per_head(top)
    total = per_head(total)
    stats = jnp.concatenate(
        [top, total, jnp.zeros((requests, tree_len, head_size - 2 * local_heads), jnp.float32)],
        axis=-1,
    )
    packed = lax.dynamic_update_slice(numerator, stats[:, :, None, :], (0, 0, local_heads, 0))
    packed = packed.reshape(seq_size, rows // seq_size, local_heads + 1, head_size)
    packed = packed.reshape(seq_size, rows // seq_size, local_heads + 1, head_size)

    def combine(stack):
        common = stack[:, :, local_heads, :local_heads]
        peak = jnp.max(common, axis=0)
        scaling = jnp.exp(common - peak)
        summed_total = jnp.sum(stack[:, :, local_heads, local_heads:2 * local_heads] * scaling,
                               axis=0)
        summed = jnp.sum(stack[:, :, :local_heads, :] * scaling[..., None], axis=0)
        stats = jnp.concatenate(
            [peak, summed_total,
             jnp.zeros(peak.shape[:-1] + (head_size - 2 * local_heads,), jnp.float32)],
            axis=-1,
        )
        return jnp.concatenate([summed, stats[:, None, :]], axis=1)

    inner = 4 if seq_size % 4 == 0 else seq_size
    outer = seq_size // inner
    hi, lo = seq_index // inner, seq_index % inner
    grouped = packed.reshape(outer, inner, rows // seq_size, local_heads + 1, head_size)
    stage = [lax.dynamic_index_in_dim(grouped, lo, 1, keepdims=False)]
    for shift in range(1, inner):
        pairs = [(h * inner + l, h * inner + (l + shift) % inner)
                 for h in range(outer) for l in range(inner)]
        target = (lo + shift) % inner
        stage.append(lax.ppermute(
            lax.dynamic_index_in_dim(grouped, target, 1, keepdims=False), "seq", pairs))
    partial = jnp.stack(
        [combine(jnp.stack([piece[h] for piece in stage], axis=0)) for h in range(outer)], axis=0
    )
    final = [lax.dynamic_index_in_dim(partial, hi, 0, keepdims=False)]
    for shift in range(1, outer):
        pairs = [(h * inner + l, ((h + shift) % outer) * inner + l)
                 for h in range(outer) for l in range(inner)]
        target = (hi + shift) % outer
        final.append(lax.ppermute(
            lax.dynamic_index_in_dim(partial, target, 0, keepdims=False), "seq", pairs))
    mine = combine(jnp.stack(final, axis=0))
    summed = mine[:, :local_heads, :]
    summed_total = mine[:, local_heads, local_heads:2 * local_heads]
    mine_attended = (summed / summed_total[..., None]).astype(jnp.bfloat16)
    across = [mine_attended]
    for shift in range(1, outer):
        pairs = [(h * inner + l, ((h + shift) % outer) * inner + l)
                 for h in range(outer) for l in range(inner)]
        across.append(lax.ppermute(mine_attended, "seq", pairs))
    by_outer = jnp.zeros((outer,) + mine_attended.shape, jnp.bfloat16)
    for shift, piece in enumerate(across):
        by_outer = lax.dynamic_update_index_in_dim(by_outer, piece, (hi - shift) % outer, 0)
    gathered = jnp.zeros((outer, inner) + mine_attended.shape, jnp.bfloat16)
    gathered = lax.dynamic_update_index_in_dim(gathered, by_outer, lo, 1)
    for shift in range(1, inner):
        pairs = [(h * inner + l, h * inner + (l + shift) % inner)
                 for h in range(outer) for l in range(inner)]
        got_piece = lax.ppermute(by_outer, "seq", pairs)
        gathered = lax.dynamic_update_index_in_dim(gathered, got_piece, (lo - shift) % inner, 1)
    attended = gathered
    attended = attended.reshape(requests * tree_len, local_heads * head_size)
    terms = jnp.dot(attended, out_weight, preferred_element_type=jnp.float32)
    head_count = lax.axis_size("head")
    if head_count & (head_count - 1):
        return lax.psum_scatter(terms, "head", scatter_dimension=1, tiled=True).astype(
            jnp.bfloat16
        )
    head_index = lax.axis_index("head")
    width = terms.shape[1] // head_count
    kept = lax.optimization_barrier(terms).reshape(rows, head_count, width)
    bit = 1
    while bit < head_count:
        mine_bit = (head_index // bit) % 2
        halves = kept.reshape(rows, kept.shape[1] // 2, 2, width)
        keep = lax.dynamic_index_in_dim(halves, mine_bit, 2, keepdims=False)
        send = lax.dynamic_index_in_dim(halves, 1 - mine_bit, 2, keepdims=False)
        kept = keep + lax.ppermute(send, "head", [(i, i ^ bit) for i in range(head_count)])
        bit *= 2
    return kept.reshape(rows, width).astype(jnp.bfloat16)


def solution(mesh):
    return jax.shard_map(
        local,
        mesh=mesh,
        in_specs=(
            P(None, None, "head", None),
            P(None, "seq", "head", None),
            P(None, "seq", "head", None),
            P(),
            P(),
            P(None, "seq", "head", None),
            P(None, "seq", "head", None),
            P("head", "seq"),
        ),
        out_specs=P(None, ("seq", "head")),
        check_vma=False,
    )
```
